32 devices in a mesh: row: 8 (over z, y), col: 4 (over x, core).
Axes of the slice: x: 2, y: 2, z: 4, core: 2. Of those that a mesh axis runs over, the one named last changes fastest.
Arguments:
- tokens: bfloat16 [2048, 4096], P('row', 'col'), may hold values from -6 to 6
- cotangent: bfloat16 [2048, 4096], P('row', 'col'), may hold values from -1.25 to 1.25
- w_up: float32 [4096, 12288], P('row', 'col'), may hold values from -0.1875 to 0.1875
- w_down: float32 [4096, 12288], P('row', 'col'), may hold values from -0.109375 to 0.109375
- mask_up: int32 [32, 96], P('row', 'col'), may hold values from 0 to 1, as said below
- mask_down: int32 [32, 96], P('row', 'col'), may hold values from 0 to 1, as said below
- moment_up: float32 [4096, 12288], P('row', 'col'), may hold values from -1.5 to 1.5
- second_up: float32 [4096, 12288], P('row', 'col'), may hold values from 0.01 to 0.2
- moment_down: float32 [4096, 12288], P('row', 'col'), may hold values from -1.5 to 1.5
- second_down: float32 [4096, 12288], P('row', 'col'), may hold values from 0.01 to 0.2
Outputs:
- token_grad: bfloat16 [2048, 4096], P('row', 'col')
- new_up: float32 [4096, 12288], P('row', 'col')
- new_moment_up: float32 [4096, 12288], P('row', 'col')
- new_second_up: float32 [4096, 12288], P('row', 'col')
- new_down: float32 [4096, 12288], P('row', 'col')
- new_moment_down: float32 [4096, 12288], P('row', 'col')
- new_second_down: float32 [4096, 12288], P('row', 'col')
The draws below stay inside these ranges and needn't reach their ends.
Inputs may be any that keep to these rules, and one draw needn't show every extreme that they name: `mask_up`: 1 where the 128 x 128 block of the up projection is kept, else 0. Each tile of 4 x 24 blocks (the blocks of one device) holds at least 1 and at most 48 kept blocks, and some tile holds exactly 48. `mask_down`: 1 where the 128 x 128 block of the down projection is kept, else 0. Each tile of 4 x 24 blocks (the blocks of one device) holds at least 1 and at most 48 kept blocks, and some tile holds exactly 48.
All inputs are finite; a program needn't handle non-finite values.
Results may differ from the reference program's by a relative error of at most 0.018.
Values may be sent and summed in bfloat16 or wider, within the bound.
No kernel may reach another device: no remote copies, remote signals or barrier semaphores. Data moves between devices by JAX's collectives and lax.ppermute only.
A program may use at most 320 MiB of HBM per device.

```python
import math
import jax
import jax.numpy as jnp
from jax import lax

D = 4096
FF = 12288
BLOCK = 128
TOKENS = 2048
DB = 32
FB = 96
DBT = 4
FBT = 24
N_ROW = 8
N_COL = 4


def tiled_mask(key):
    tile_rows = DB // DBT
    tile_cols = FB // FBT
    tiles = tile_rows * tile_cols
    per_tile = DBT * FBT
    most = per_tile // 2
    count_key, pick_key, rank_key = jax.random.split(key, 3)
    counts = jax.random.randint(count_key, (tiles,), 1, most + 1)
    fullest = jax.random.randint(pick_key, (), 0, tiles)
    counts = jnp.where(jnp.arange(tiles) == fullest, most, counts)
    rank_keys = jax.random.split(rank_key, tiles)
    ranks = jax.vmap(lambda k: jax.random.permutation(k, per_tile))(rank_keys)
    kept = jnp.where(ranks < counts[:, None], 1, 0)
    kept = kept.reshape(tile_rows, tile_cols, DBT, FBT).transpose(0, 2, 1, 3)
    return kept.reshape(DB, FB).astype(jnp.int32)


def draw_mask_up(key, part):
    return tiled_mask(jax.random.fold_in(key, 11))


def draw_mask_down(key, part):
    return tiled_mask(jax.random.fold_in(key, 23))


def shard_levels(rng, extent, cuts, low, top_value):
    gain, own = 1.0, jax.random.fold_in(rng, 6)
    for dim, parts in cuts:
        steps = jnp.exp(jax.random.uniform(jax.random.fold_in(own, dim), (parts,), jnp.float32, low / len(cuts), top_value / len(cuts)))
        gain = gain * jnp.repeat(steps, extent[dim] // parts).reshape([-1 if axis == dim else 1 for axis in range(len(extent))])
    return gain


def gaussian(own_key, shape, scale, limit, cuts=(), kind=jnp.bfloat16):
    drawn = jax.random.normal(own_key, shape, jnp.float32) * scale
    if len(cuts) > 0:
        drawn = shard_levels(own_key, shape, cuts, -0.22, 0.18) * drawn
    return jnp.clip(drawn, min=-limit, max=limit).astype(kind)


def setup_inputs(seed: int = 0) -> dict:
    keys = jax.random.split(jax.random.key(seed), 11)
    tokens = gaussian(keys[0], (TOKENS, D), 1.0, 6.0, ((0, 8), (1, 4)))
    cotangent = gaussian(keys[1], (TOKENS, D), (4.0 / TOKENS ** 0.5), 1.25, ((0, 8), (1, 4)))
    w_up = gaussian(keys[2], (D, FF), (D // 4) ** -0.5, 0.1875, ((0, 8), (1, 4)), jnp.float32)
    w_down = gaussian(keys[3], (D, FF), (FF // 4) ** -0.5, 0.109375, ((0, 8), (1, 4)), jnp.float32)
    mask_up = draw_mask_up(jax.random.fold_in(keys[10], 71), 0)
    mask_down = draw_mask_down(jax.random.fold_in(keys[10], 71), 0)
    moment_up = gaussian(keys[6], (D, FF), 0.1, 1.5, ((0, 8), (1, 4)), jnp.float32)
    second_up = jnp.clip(jnp.exp(math.log(0.2) - 2.9957323 * jax.random.uniform(keys[7], (D, FF), jnp.float32) ** shard_levels(keys[7], (D, FF), ((0, 8), (1, 4)), -0.2, 0.2)), 0.01, 0.2)
    moment_down = gaussian(keys[8], (D, FF), 0.1, 1.5, ((0, 8), (1, 4)), jnp.float32)
    second_down = jnp.clip(jnp.exp(math.log(0.2) - 2.9957323 * jax.random.uniform(keys[9], (D, FF), jnp.float32) ** shard_levels(keys[9], (D, FF), ((0, 8), (1, 4)), -0.2, 0.2)), 0.01, 0.2)
    return dict(tokens=tokens, cotangent=cotangent, w_up=w_up, w_down=w_down, mask_up=mask_up, mask_down=mask_down, moment_up=moment_up, second_up=second_up, moment_down=moment_down, second_down=second_down)


inv_root_two = 0.7071067811865476
inv_root_two_pi = 0.3989422804014327
learn_rate = 0.001
bias_first = 1.0 - 0.9 ** 10
bias_second = 1.0 - 0.95 ** 10

def expand_mask(mask, block):
    blocks_r, blocks_c = mask.shape
    values = mask.astype(jnp.float32)[:, None, :, None]
    values = jnp.broadcast_to(values, (blocks_r, block, blocks_c, block))
    return values.reshape(blocks_r * block, blocks_c * block)

def gelu_parts(preact):
    normal_cdf = 0.5 * (1.0 + lax.erf(preact * inv_root_two))
    density = jnp.exp(-0.5 * preact * preact) * inv_root_two_pi
    return (preact * normal_cdf, normal_cdf + preact * density)

def grouped_sum(left, right, groups, axis):
    width = left.shape[axis] // groups
    out_shape = (left.shape[1 - axis], right.shape[1 - axis])

    def accumulate(total, index):
        start = (index * width).astype(jnp.int32)
        part_left = lax.dynamic_slice_in_dim(left, start, width, axis)
        part_right = lax.dynamic_slice_in_dim(right, start, width, axis)
        product = lax.dot_general(part_left, part_right, (((axis,), (axis,)), ((), ())), preferred_element_type=jnp.float32)
        rounded = lax.optimization_barrier(product.astype(jnp.bfloat16))
        return (total + rounded.astype(jnp.float32), None)
    total, _ = lax.scan(accumulate, jnp.zeros(out_shape, jnp.float32), jnp.arange(groups, dtype=jnp.int32))
    return total

def adam_update(weight, moment, second, grad):
    moment_new = 0.9 * moment + 0.1 * grad
    second_new = 0.95 * second + 0.05 * grad * grad
    step_size = moment_new / bias_first / (jnp.sqrt(second_new / bias_second) + 1e-08)
    return (weight - learn_rate * step_size, moment_new, second_new)

def reference(tokens, cotangent, w_up, w_down, mask_up, mask_down, moment_up, second_up, moment_down, second_down):
    keep_up = expand_mask(mask_up, BLOCK)
    keep_down = expand_mask(mask_down, BLOCK)
    up_used = (w_up * keep_up).astype(jnp.bfloat16)
    down_used = (w_down * keep_down).astype(jnp.bfloat16)
    preact = jnp.dot(tokens, up_used, preferred_element_type=jnp.float32)
    gelu_value, gelu_slope = gelu_parts(preact)
    activation = gelu_value.astype(jnp.bfloat16)
    act_grad = jnp.dot(cotangent, down_used, preferred_element_type=jnp.float32)
    pre_grad = (act_grad * gelu_slope).astype(jnp.bfloat16)
    token_grad = grouped_sum(pre_grad, up_used, N_COL, 1).astype(jnp.bfloat16)
    grad_up = keep_up * grouped_sum(tokens, pre_grad, N_ROW, 0)
    grad_down = keep_down * grouped_sum(cotangent, activation, N_ROW, 0)
    new_up, new_moment_up, new_second_up = adam_update(w_up, moment_up, second_up, grad_up)
    new_down, new_moment_down, new_second_down = adam_update(w_down, moment_down, second_down, grad_down)
    return (token_grad, new_up, new_moment_up, new_second_up, new_down, new_moment_down, new_second_down)
```

```python
import jax
import jax.numpy as jnp
from jax import lax
from jax.sharding import PartitionSpec as P

inv_root_two = 0.7071067811865476
inv_root_two_pi = 0.3989422804014327
learn_rate = 0.001
bias_first = 1.0 - 0.9**10
bias_second = 1.0 - 0.95**10


def expand_mask(mask, block):
    blocks_r, blocks_c = mask.shape
    values = mask.astype(jnp.float32)[:, None, :, None]
    values = jnp.broadcast_to(values, (blocks_r, block, blocks_c, block))
    return values.reshape(blocks_r * block, blocks_c * block)


def gelu_parts(preact):
    normal_cdf = 0.5 * (1.0 + lax.erf(preact * inv_root_two))
    density = jnp.exp(-0.5 * preact * preact) * inv_root_two_pi
    return (preact * normal_cdf, normal_cdf + preact * density)


def adam_update(weight, moment, second, grad):
    moment_new = 0.9 * moment + 0.1 * grad
    second_new = 0.95 * second + 0.05 * grad * grad
    step_size = moment_new / bias_first / (jnp.sqrt(second_new / bias_second) + 1e-08)
    return (weight - learn_rate * step_size, moment_new, second_new)


def token_product(rows_full, other):
    return lax.dot_general(
        rows_full, other, (((0,), (0,)), ((), ())), preferred_element_type=jnp.float32
    )


def to_blocks(dense, block):
    rows, cols = dense.shape[-2:]
    lead = dense.shape[:-2]
    nr, nc = rows // block, cols // block
    x = dense.reshape(lead + (nr, block, nc, block))
    k = len(lead)
    x = jnp.moveaxis(x, k + 2, k + 1)
    return x.reshape(lead + (nr * nc, block, block))


def from_blocks(blocks, nr, nc):
    lead = blocks.shape[:-3]
    block = blocks.shape[-1]
    x = blocks.reshape(lead + (nr, nc, block, block))
    k = len(lead)
    x = jnp.moveaxis(x, k + 1, k + 2)
    return x.reshape(lead + (nr * block, nc * block))


def kept_index(flat_mask, slots):
    n = flat_mask.shape[-1]
    upto = jnp.cumsum(flat_mask, axis=-1)
    k = jnp.arange(slots, dtype=jnp.int32)
    idx = jnp.sum((upto[..., None, :] <= k[:, None]).astype(jnp.int32), axis=-1)
    return jnp.minimum(idx, n - 1)


def slot_of(flat_mask):
    return jnp.cumsum(flat_mask, axis=-1) - flat_mask


def compact(blocks, idx):
    return jnp.take(blocks, idx, axis=-3)


def shards(
    tokens,
    cotangent,
    w_up,
    w_down,
    mask_up,
    mask_down,
    moment_up,
    second_up,
    moment_down,
    second_down,
):
    nr, nc = mask_up.shape
    block = w_up.shape[0] // nr
    slots = (nr * nc) // 2
    n_row = lax.axis_size("row")

    flat_up = mask_up.reshape(nr * nc)
    flat_down = mask_down.reshape(nr * nc)
    masks_up = lax.all_gather(flat_up, "row", axis=0)
    masks_down = lax.all_gather(flat_down, "row", axis=0)

    up_blocks = to_blocks(w_up.astype(jnp.bfloat16), block)
    down_blocks = to_blocks(w_down.astype(jnp.bfloat16), block)
    up_sent = compact(up_blocks, kept_index(flat_up, slots))
    down_sent = compact(down_blocks, kept_index(flat_down, slots))

    features, cot_rows = (
        lax.all_gather(tokens, "col", axis=1, tiled=True),
        lax.all_gather(cotangent, "col", axis=1, tiled=True),
    )

    def rebuild(sent, masks):
        got = lax.all_gather(sent, "row", axis=0)
        flat = got.reshape((n_row * slots, block, block))
        where = slot_of(masks) + (jnp.arange(n_row, dtype=jnp.int32) * slots)[:, None]
        dense = jnp.take(flat, where.reshape(-1), axis=0)
        keep = masks.reshape(-1)[:, None, None] > 0
        dense = jnp.where(keep, dense, jnp.zeros_like(dense))
        dense = dense.reshape((n_row, nr * nc, block, block))
        dense = from_blocks(dense, nr, nc)
        return dense.reshape((n_row * nr * block, nc * block))

    up_whole = rebuild(up_sent, masks_up)
    down_whole = rebuild(down_sent, masks_down)

    preact = jnp.dot(features, up_whole, preferred_element_type=jnp.float32)
    act_grad = jnp.dot(cot_rows, down_whole, preferred_element_type=jnp.float32)
    gelu_value, gelu_slope = gelu_parts(preact)
    activation = gelu_value.astype(jnp.bfloat16)
    pre_grad = (act_grad * gelu_slope).astype(jnp.bfloat16)
    partial_tokens = lax.dot_general(
        pre_grad, up_whole, (((1,), (1,)), ((), ())), preferred_element_type=jnp.float32
    )

    def reduce_kept(partial, masks, own):
        blocks = to_blocks(
            partial.astype(jnp.bfloat16).reshape((n_row, nr * block, nc * block)), block
        )
        idx = kept_index(masks, slots)
        sent = jnp.take_along_axis(blocks, idx[:, :, None, None], axis=1)
        summed = lax.psum_scatter(sent, "row", scatter_dimension=0, tiled=True)[0]
        dense = jnp.take(summed, slot_of(own), axis=0)
        keep = own[:, None, None] > 0
        dense = jnp.where(keep, dense.astype(jnp.float32), jnp.zeros(dense.shape, jnp.float32))
        return from_blocks(dense, nr, nc)

    grad_down = reduce_kept(token_product(cot_rows, activation), masks_down, flat_down)
    grad_up = reduce_kept(token_product(features, pre_grad), masks_up, flat_up)
    token_grad = lax.psum_scatter(
        partial_tokens.astype(jnp.bfloat16), "col", scatter_dimension=1, tiled=True
    )
    new_up, new_moment_up, new_second_up = adam_update(w_up, moment_up, second_up, grad_up)
    new_down, new_moment_down, new_second_down = adam_update(
        w_down, moment_down, second_down, grad_down
    )
    return (
        token_grad,
        new_up,
        new_moment_up,
        new_second_up,
        new_down,
        new_moment_down,
        new_second_down,
    )


def solution(mesh):
    spec = P("row", "col")
    return jax.shard_map(
        shards,
        mesh=mesh,
        in_specs=(spec,) * 10,
        out_specs=(spec,) * 7,
        check_vma=False,
    )
```

```python
import jax
import jax.numpy as jnp
from jax import lax
from jax.sharding import PartitionSpec as P

inv_root_two = 0.7071067811865476
inv_root_two_pi = 0.3989422804014327
learn_rate = 0.001
bias_first = 1.0 - 0.9**10
bias_second = 1.0 - 0.95**10


def expand_mask(mask, block):
    blocks_r, blocks_c = mask.shape
    values = mask.astype(jnp.float32)[:, None, :, None]
    values = jnp.broadcast_to(values, (blocks_r, block, blocks_c, block))
    return values.reshape(blocks_r * block, blocks_c * block)


def gelu_parts(preact):
    normal_cdf = 0.5 * (1.0 + lax.erf(preact * inv_root_two))
    density = jnp.exp(-0.5 * preact * preact) * inv_root_two_pi
    return (preact * normal_cdf, normal_cdf + preact * density)


def adam_update(weight, moment, second, grad):
    moment_new = 0.9 * moment + 0.1 * grad
    second_new = 0.95 * second + 0.05 * grad * grad
    step_size = moment_new / bias_first / (jnp.sqrt(second_new / bias_second) + 1e-08)
    return (weight - learn_rate * step_size, moment_new, second_new)


def token_product(rows_full, other):
    return lax.dot_general(
        rows_full, other, (((0,), (0,)), ((), ())), preferred_element_type=jnp.float32
    )


def to_blocks(dense, block):
    rows, cols = dense.shape[-2:]
    lead = dense.shape[:-2]
    nr, nc = rows // block, cols // block
    x = dense.reshape(lead + (nr, block, nc, block))
    k = len(lead)
    x = jnp.moveaxis(x, k + 2, k + 1)
    return x.reshape(lead + (nr * nc, block, block))


def from_blocks(blocks, nr, nc):
    lead = blocks.shape[:-3]
    block = blocks.shape[-1]
    x = blocks.reshape(lead + (nr, nc, block, block))
    k = len(lead)
    x = jnp.moveaxis(x, k + 1, k + 2)
    return x.reshape(lead + (nr * block, nc * block))


def kept_index(flat_mask, slots):
    n = flat_mask.shape[-1]
    upto = jnp.cumsum(flat_mask, axis=-1)
    k = jnp.arange(slots, dtype=jnp.int32)
    idx = jnp.sum((upto[..., None, :] <= k[:, None]).astype(jnp.int32), axis=-1)
    return jnp.minimum(idx, n - 1)


def slot_of(flat_mask):
    return jnp.cumsum(flat_mask, axis=-1) - flat_mask


def shards(
    tokens,
    cotangent,
    w_up,
    w_down,
    mask_up,
    mask_down,
    moment_up,
    second_up,
    moment_down,
    second_down,
):
    nr, nc = mask_up.shape
    nb = nr * nc
    block = w_up.shape[0] // nr
    slots = nb // 2
    n_row = lax.axis_size("row")
    width = 2 * slots + 2
    zero_slot = 2 * slots
    mask_slot = 2 * slots + 1

    flat_up = mask_up.reshape(nb)
    flat_down = mask_down.reshape(nb)

    def pick(w, flat):
        blocks = to_blocks(w.astype(jnp.bfloat16), block)
        return blocks.at[kept_index(flat, slots)].get(mode="promise_in_bounds")

    mask_rows = jnp.zeros((block, block), jnp.bfloat16)
    mask_rows = mask_rows.at[0, :nb].set(flat_up.astype(jnp.bfloat16))
    mask_rows = mask_rows.at[1, :nb].set(flat_down.astype(jnp.bfloat16))
    sent = jnp.concatenate(
        [
            pick(w_up, flat_up),
            pick(w_down, flat_down),
            jnp.zeros((1, block, block), jnp.bfloat16),
            mask_rows[None],
        ],
        axis=0,
    )
    got = lax.all_gather(sent, "row", axis=0)
    masks_up = got[:, mask_slot, 0, :nb].astype(jnp.int32)
    masks_down = got[:, mask_slot, 1, :nb].astype(jnp.int32)
    flat_got = got.reshape((n_row * width, block, block))

    features, cot_rows = (
        lax.all_gather(tokens, "col", axis=1, tiled=True),
        lax.all_gather(cotangent, "col", axis=1, tiled=True),
    )

    def rebuild(masks, offset):
        base = (jnp.arange(n_row, dtype=jnp.int32) * width)[:, None]
        where = jnp.where(masks > 0, base + offset + slot_of(masks), base + zero_slot)
        dense = flat_got.at[where.reshape(-1)].get(mode="promise_in_bounds")
        dense = dense.reshape((n_row, nb, block, block))
        dense = from_blocks(dense, nr, nc)
        return dense.reshape((n_row * nr * block, nc * block))

    up_whole = rebuild(masks_up, 0)
    down_whole = rebuild(masks_down, slots)

    preact = jnp.dot(features, up_whole, preferred_element_type=jnp.float32)
    act_grad = jnp.dot(cot_rows, down_whole, preferred_element_type=jnp.float32)
    gelu_value, gelu_slope = gelu_parts(preact)
    activation = gelu_value.astype(jnp.bfloat16)
    pre_grad = (act_grad * gelu_slope).astype(jnp.bfloat16)
    partial_tokens = lax.dot_general(
        pre_grad, up_whole, (((1,), (1,)), ((), ())), preferred_element_type=jnp.float32
    )

    def reduce_kept(partial, masks, own):
        view = partial.astype(jnp.bfloat16).reshape((n_row * nr, block, nc, block))
        idx = kept_index(masks, slots)
        rows = (jnp.arange(n_row, dtype=jnp.int32) * nr)[:, None] + idx // nc
        cols = idx % nc
        sent = view.at[rows, :, cols, :].get(mode="promise_in_bounds")
        summed = lax.psum_scatter(sent, "row", scatter_dimension=0, tiled=True)[0]
        dense = summed.at[slot_of(own)].get(mode="promise_in_bounds")
        keep = own[:, None, None] > 0
        dense = jnp.where(keep, dense.astype(jnp.float32), jnp.zeros(dense.shape, jnp.float32))
        return from_blocks(dense, nr, nc)

    grad_down = reduce_kept(token_product(cot_rows, activation), masks_down, flat_down)
    grad_up = reduce_kept(token_product(features, pre_grad), masks_up, flat_up)
    token_grad = lax.psum_scatter(
        partial_tokens.astype(jnp.bfloat16), "col", scatter_dimension=1, tiled=True
    )
    new_up, new_moment_up, new_second_up = adam_update(w_up, moment_up, second_up, grad_up)
    new_down, new_moment_down, new_second_down = adam_update(
        w_down, moment_down, second_down, grad_down
    )
    return (
        token_grad,
        new_up,
        new_moment_up,
        new_second_up,
        new_down,
        new_moment_down,
        new_second_down,
    )


def solution(mesh):
    spec = P("row", "col")
    return jax.shard_map(
        shards,
        mesh=mesh,
        in_specs=(spec,) * 10,
        out_specs=(spec,) * 7,
        check_vma=False,
    )
```

```python
import jax
import jax.numpy as jnp
from jax import lax
from jax.sharding import PartitionSpec as P

inv_root_two = 0.7071067811865476
inv_root_two_pi = 0.3989422804014327
learn_rate = 0.001
bias_first = 1.0 - 0.9**10
bias_second = 1.0 - 0.95**10


def expand_mask(mask, block):
    blocks_r, blocks_c = mask.shape
    values = mask.astype(jnp.float32)[:, None, :, None]
    values = jnp.broadcast_to(values, (blocks_r, block, blocks_c, block))
    return values.reshape(blocks_r * block, blocks_c * block)


def gelu_parts(preact):
    normal_cdf = 0.5 * (1.0 + lax.erf(preact * inv_root_two))
    density = jnp.exp(-0.5 * preact * preact) * inv_root_two_pi
    return (preact * normal_cdf, normal_cdf + preact * density)


def adam_update(weight, moment, second, grad):
    moment_new = 0.9 * moment + 0.1 * grad
    second_new = 0.95 * second + 0.05 * grad * grad
    step_size = moment_new / bias_first / (jnp.sqrt(second_new / bias_second) + 1e-08)
    return (weight - learn_rate * step_size, moment_new, second_new)


def token_product(rows_full, other):
    return lax.dot_general(
        rows_full, other, (((0,), (0,)), ((), ())), preferred_element_type=jnp.float32
    )


def to_blocks(dense, block):
    rows, cols = dense.shape[-2:]
    lead = dense.shape[:-2]
    nr, nc = rows // block, cols // block
    x = dense.reshape(lead + (nr, block, nc, block))
    k = len(lead)
    x = jnp.moveaxis(x, k + 2, k + 1)
    return x.reshape(lead + (nr * nc, block, block))


def from_blocks(blocks, nr, nc):
    lead = blocks.shape[:-3]
    block = blocks.shape[-1]
    x = blocks.reshape(lead + (nr, nc, block, block))
    k = len(lead)
    x = jnp.moveaxis(x, k + 1, k + 2)
    return x.reshape(lead + (nr * block, nc * block))


def kept_index(flat_mask, slots):
    n = flat_mask.shape[-1]
    upto = jnp.cumsum(flat_mask, axis=-1)
    k = jnp.arange(slots, dtype=jnp.int32)
    idx = jnp.sum((upto[..., None, :] <= k[:, None]).astype(jnp.int32), axis=-1)
    return jnp.minimum(idx, n - 1)


def slot_of(flat_mask):
    return jnp.cumsum(flat_mask, axis=-1) - flat_mask


def shards(
    tokens,
    cotangent,
    w_up,
    w_down,
    mask_up,
    mask_down,
    moment_up,
    second_up,
    moment_down,
    second_down,
):
    nr, nc = mask_up.shape
    nb = nr * nc
    block = w_up.shape[0] // nr
    slots = nb // 2
    n_row = lax.axis_size("row")
    me = lax.axis_index("row")
    width = slots + 2
    zero_slot = slots
    mask_slot = slots + 1
    rows_n = jnp.arange(n_row, dtype=jnp.int32)

    flat_up = mask_up.reshape(nb)
    flat_down = mask_down.reshape(nb)

    def package(w, flat):
        blocks = to_blocks(w.astype(jnp.bfloat16), block)
        kept = blocks.at[kept_index(flat, slots)].get(mode="promise_in_bounds")
        mask_rows = jnp.zeros((block, block), jnp.bfloat16)
        mask_rows = mask_rows.at[0, :nb].set(flat.astype(jnp.bfloat16))
        return jnp.concatenate(
            [kept, jnp.zeros((1, block, block), jnp.bfloat16), mask_rows[None]], axis=0
        )

    def shift_perm(s):
        return [(i, (i + s) % n_row) for i in range(n_row)]

    got_up = lax.all_gather(package(w_up, flat_up), "row", axis=0)
    sent_down = package(w_down, flat_down)
    got_down = jnp.stack(
        [sent_down]
        + [lax.ppermute(sent_down, "row", shift_perm(s)) for s in range(1, n_row)]
    )
    pos_down = (me - rows_n) % n_row
    masks_up = got_up[:, mask_slot, 0, :nb].astype(jnp.int32)
    masks_down = got_down[pos_down, mask_slot, 0, :nb].astype(jnp.int32)

    features, cot_rows = (
        lax.all_gather(tokens, "col", axis=1, tiled=True),
        lax.all_gather(cotangent, "col", axis=1, tiled=True),
    )

    def rebuild(got, masks, pos):
        flat_got = got.reshape((n_row * width, block, block))
        base = (pos * width)[:, None]
        where = jnp.where(masks > 0, base + slot_of(masks), base + zero_slot)
        dense = flat_got.at[where.reshape(-1)].get(mode="promise_in_bounds")
        dense = dense.reshape((n_row, nb, block, block))
        dense = from_blocks(dense, nr, nc)
        return dense.reshape((n_row * nr * block, nc * block))

    up_whole = rebuild(got_up, masks_up, rows_n)
    down_whole = rebuild(got_down, masks_down, pos_down)

    preact = jnp.dot(features, up_whole, preferred_element_type=jnp.float32)
    act_grad = jnp.dot(cot_rows, down_whole, preferred_element_type=jnp.float32)
    gelu_value, gelu_slope = gelu_parts(preact)
    activation = gelu_value.astype(jnp.bfloat16)
    pre_grad = (act_grad * gelu_slope).astype(jnp.bfloat16)
    partial_tokens = lax.dot_general(
        pre_grad, up_whole, (((1,), (1,)), ((), ())), preferred_element_type=jnp.float32
    )

    def kept_blocks(partial, masks, dest):
        view = partial.astype(jnp.bfloat16).reshape((n_row * nr, block, nc, block))
        idx = kept_index(masks, slots)
        rows = (dest * nr)[:, None] + idx // nc
        cols = idx % nc
        return view.at[rows, :, cols, :].get(mode="promise_in_bounds")

    def unpack(summed, own):
        dense = summed.at[slot_of(own)].get(mode="promise_in_bounds")
        keep = own[:, None, None] > 0
        dense = jnp.where(keep, dense.astype(jnp.float32), jnp.zeros(dense.shape, jnp.float32))
        return from_blocks(dense, nr, nc)

    sent = kept_blocks(token_product(cot_rows, activation), masks_down, rows_n)
    grad_down = unpack(lax.psum_scatter(sent, "row", scatter_dimension=0, tiled=True)[0], flat_down)
    dest = (me + rows_n) % n_row
    sent = kept_blocks(token_product(features, pre_grad), masks_up[dest], dest)
    total = sent[0].astype(jnp.float32)
    for s in range(1, n_row):
        total = total + lax.ppermute(sent[s], "row", shift_perm(s)).astype(jnp.float32)
    grad_up = unpack(total, flat_up)

    token_grad = lax.psum_scatter(
        partial_tokens.astype(jnp.bfloat16), "col", scatter_dimension=1, tiled=True
    )
    new_up, new_moment_up, new_second_up = adam_update(w_up, moment_up, second_up, grad_up)
    new_down, new_moment_down, new_second_down = adam_update(
        w_down, moment_down, second_down, grad_down
    )
    return (
        token_grad,
        new_up,
        new_moment_up,
        new_second_up,
        new_down,
        new_moment_down,
        new_second_down,
    )


def solution(mesh):
    spec = P("row", "col")
    return jax.shard_map(
        shards,
        mesh=mesh,
        in_specs=(spec,) * 10,
        out_specs=(spec,) * 7,
        check_vma=False,
    )
```

```python
import jax
import jax.numpy as jnp
from jax import lax
from jax.sharding import PartitionSpec as P

inv_root_two = 0.7071067811865476
inv_root_two_pi = 0.3989422804014327
learn_rate = 0.001
bias_first = 1.0 - 0.9**10
bias_second = 1.0 - 0.95**10


def expand_mask(mask, block):
    blocks_r, blocks_c = mask.shape
    values = mask.astype(jnp.float32)[:, None, :, None]
    values = jnp.broadcast_to(values, (blocks_r, block, blocks_c, block))
    return values.reshape(blocks_r * block, blocks_c * block)


def gelu_parts(preact):
    normal_cdf = 0.5 * (1.0 + lax.erf(preact * inv_root_two))
    density = jnp.exp(-0.5 * preact * preact) * inv_root_two_pi
    return (preact * normal_cdf, normal_cdf + preact * density)


def adam_update(weight, moment, second, grad):
    moment_new = 0.9 * moment + 0.1 * grad
    second_new = 0.95 * second + 0.05 * grad * grad
    step_size = moment_new / bias_first / (jnp.sqrt(second_new / bias_second) + 1e-08)
    return (weight - learn_rate * step_size, moment_new, second_new)


def token_product(rows_full, other):
    return lax.dot_general(
        rows_full, other, (((0,), (0,)), ((), ())), preferred_element_type=jnp.float32
    )


def to_blocks(dense, block):
    rows, cols = dense.shape[-2:]
    lead = dense.shape[:-2]
    nr, nc = rows // block, cols // block
    x = dense.reshape(lead + (nr, block, nc, block))
    k = len(lead)
    x = jnp.moveaxis(x, k + 2, k + 1)
    return x.reshape(lead + (nr * nc, block, block))


def from_blocks(blocks, nr, nc):
    lead = blocks.shape[:-3]
    block = blocks.shape[-1]
    x = blocks.reshape(lead + (nr, nc, block, block))
    k = len(lead)
    x = jnp.moveaxis(x, k + 1, k + 2)
    return x.reshape(lead + (nr * block, nc * block))


def kept_index(flat_mask, slots):
    n = flat_mask.shape[-1]
    upto = jnp.cumsum(flat_mask, axis=-1)
    k = jnp.arange(slots, dtype=jnp.int32)
    idx = jnp.sum((upto[..., None, :] <= k[:, None]).astype(jnp.int32), axis=-1)
    return jnp.minimum(idx, n - 1)


def slot_of(flat_mask):
    return jnp.cumsum(flat_mask, axis=-1) - flat_mask


def shards(
    tokens,
    cotangent,
    w_up,
    w_down,
    mask_up,
    mask_down,
    moment_up,
    second_up,
    moment_down,
    second_down,
):
    nr, nc = mask_up.shape
    nb = nr * nc
    block = w_up.shape[0] // nr
    slots = nb // 2
    n_row = lax.axis_size("row")
    width = slots + 2
    zero_slot = slots
    mask_slot = slots + 1
    rows_n = jnp.arange(n_row, dtype=jnp.int32)

    flat_up = mask_up.reshape(nb)
    flat_down = mask_down.reshape(nb)

    def package(w, flat):
        blocks = to_blocks(w.astype(jnp.bfloat16), block)
        kept = blocks.at[kept_index(flat, slots)].get(mode="promise_in_bounds")
        mask_rows = jnp.zeros((block, block), jnp.bfloat16)
        mask_rows = mask_rows.at[0, :nb].set(flat.astype(jnp.bfloat16))
        return jnp.concatenate(
            [kept, jnp.zeros((1, block, block), jnp.bfloat16), mask_rows[None]], axis=0
        )

    got_up = lax.all_gather(package(w_up, flat_up), "row", axis=0)
    got_down = lax.all_gather(package(w_down, flat_down), "row", axis=0)
    masks_up = got_up[:, mask_slot, 0, :nb].astype(jnp.int32)
    masks_down = got_down[:, mask_slot, 0, :nb].astype(jnp.int32)

    features, cot_rows = (
        lax.all_gather(tokens, "col", axis=1, tiled=True),
        lax.all_gather(cotangent, "col", axis=1, tiled=True),
    )

    def rebuild(got, masks, pos):
        flat_got = got.reshape((n_row * width, block, block))
        base = (pos * width)[:, None]
        where = jnp.where(masks > 0, base + slot_of(masks), base + zero_slot)
        dense = flat_got.at[where.reshape(-1)].get(mode="promise_in_bounds")
        dense = dense.reshape((n_row, nb, block, block))
        dense = from_blocks(dense, nr, nc)
        return dense.reshape((n_row * nr * block, nc * block))

    up_whole = rebuild(got_up, masks_up, rows_n)
    down_whole = rebuild(got_down, masks_down, rows_n)

    preact = jnp.dot(features, up_whole, preferred_element_type=jnp.float32)
    act_grad = jnp.dot(cot_rows, down_whole, preferred_element_type=jnp.float32)
    gelu_value, gelu_slope = gelu_parts(preact)
    activation = gelu_value.astype(jnp.bfloat16)
    pre_grad = (act_grad * gelu_slope).astype(jnp.bfloat16)
    partial_tokens = lax.dot_general(
        pre_grad, up_whole, (((1,), (1,)), ((), ())), preferred_element_type=jnp.float32
    )

    def kept_blocks(partial, masks, dest):
        view = partial.astype(jnp.bfloat16).reshape((n_row * nr, block, nc, block))
        idx = kept_index(masks, slots)
        rows = (dest * nr)[:, None] + idx // nc
        cols = idx % nc
        return view.at[rows, :, cols, :].get(mode="promise_in_bounds")

    def unpack(summed, own):
        dense = summed.at[slot_of(own)].get(mode="promise_in_bounds")
        keep = own[:, None, None] > 0
        dense = jnp.where(keep, dense.astype(jnp.float32), jnp.zeros(dense.shape, jnp.float32))
        return from_blocks(dense, nr, nc)

    def reduce_kept(partial, masks, own):
        sent = kept_blocks(partial, masks, rows_n)
        return unpack(lax.psum_scatter(sent, "row", scatter_dimension=0, tiled=True)[0], own)

    grad_down = reduce_kept(token_product(cot_rows, activation), masks_down, flat_down)
    grad_up = reduce_kept(token_product(features, pre_grad), masks_up, flat_up)

    token_grad = lax.psum_scatter(
        partial_tokens.astype(jnp.bfloat16), "col", scatter_dimension=1, tiled=True
    )
    new_up, new_moment_up, new_second_up = adam_update(w_up, moment_up, second_up, grad_up)
    new_down, new_moment_down, new_second_down = adam_update(
        w_down, moment_down, second_down, grad_down
    )
    return (
        token_grad,
        new_up,
        new_moment_up,
        new_second_up,
        new_down,
        new_moment_down,
        new_second_down,
    )


def solution(mesh):
    spec = P("row", "col")
    return jax.shard_map(
        shards,
        mesh=mesh,
        in_specs=(spec,) * 10,
        out_specs=(spec,) * 7,
        check_vma=False,
    )
```

```python
import jax
import jax.numpy as jnp
from jax import lax
from jax.sharding import PartitionSpec as P

inv_root_two = 0.7071067811865476
inv_root_two_pi = 0.3989422804014327
learn_rate = 0.001
bias_first = 1.0 - 0.9**10
bias_second = 1.0 - 0.95**10


def expand_mask(mask, block):
    blocks_r, blocks_c = mask.shape
    values = mask.astype(jnp.float32)[:, None, :, None]
    values = jnp.broadcast_to(values, (blocks_r, block, blocks_c, block))
    return values.reshape(blocks_r * block, blocks_c * block)


def gelu_parts(preact):
    normal_cdf = 0.5 * (1.0 + lax.erf(preact * inv_root_two))
    density = jnp.exp(-0.5 * preact * preact) * inv_root_two_pi
    return (preact * normal_cdf, normal_cdf + preact * density)


def adam_update(weight, moment, second, grad):
    moment_new = 0.9 * moment + 0.1 * grad
    second_new = 0.95 * second + 0.05 * grad * grad
    step_size = moment_new / bias_first / (jnp.sqrt(second_new / bias_second) + 1e-08)
    return (weight - learn_rate * step_size, moment_new, second_new)


def token_product(rows_full, other):
    return lax.dot_general(
        rows_full, other, (((0,), (0,)), ((), ())), preferred_element_type=jnp.float32
    )


def to_blocks(dense, block):
    rows, cols = dense.shape[-2:]
    lead = dense.shape[:-2]
    nr, nc = rows // block, cols // block
    x = dense.reshape(lead + (nr, block, nc, block))
    k = len(lead)
    x = jnp.moveaxis(x, k + 2, k + 1)
    return x.reshape(lead + (nr * nc, block, block))


def from_blocks(blocks, nr, nc):
    lead = blocks.shape[:-3]
    block = blocks.shape[-1]
    x = blocks.reshape(lead + (nr, nc, block, block))
    k = len(lead)
    x = jnp.moveaxis(x, k + 1, k + 2)
    return x.reshape(lead + (nr * block, nc * block))


def kept_index(flat_mask, slots):
    n = flat_mask.shape[-1]
    upto = jnp.cumsum(flat_mask, axis=-1)
    k = jnp.arange(slots, dtype=jnp.int32)
    idx = jnp.sum((upto[..., None, :] <= k[:, None]).astype(jnp.int32), axis=-1)
    return jnp.minimum(idx, n - 1)


def slot_of(flat_mask):
    return jnp.cumsum(flat_mask, axis=-1) - flat_mask


def shards(
    tokens,
    cotangent,
    w_up,
    w_down,
    mask_up,
    mask_down,
    moment_up,
    second_up,
    moment_down,
    second_down,
):
    nr, nc = mask_up.shape
    nb = nr * nc
    block = w_up.shape[0] // nr
    slots = nb // 2
    n_row = lax.axis_size("row")
    width = slots + 2
    zero_slot = slots
    mask_slot = slots + 1
    rows_n = jnp.arange(n_row, dtype=jnp.int32)

    flat_up = mask_up.reshape(nb)
    flat_down = mask_down.reshape(nb)

    def package(w, flat):
        blocks = to_blocks(w.astype(jnp.bfloat16), block)
        kept = blocks.at[kept_index(flat, slots)].get(mode="promise_in_bounds")
        mask_rows = jnp.zeros((block, block), jnp.bfloat16)
        mask_rows = mask_rows.at[0, :nb].set(flat_up.astype(jnp.bfloat16))
        mask_rows = mask_rows.at[1, :nb].set(flat_down.astype(jnp.bfloat16))
        return jnp.concatenate(
            [kept, jnp.zeros((1, block, block), jnp.bfloat16), mask_rows[None]], axis=0
        )

    got_up = lax.all_gather(package(w_up, flat_up), "row", axis=0)
    got_down = lax.all_gather(package(w_down, flat_down), "row", axis=0)
    masks_up = got_up[:, mask_slot, 0, :nb].astype(jnp.int32)
    masks_down = got_up[:, mask_slot, 1, :nb].astype(jnp.int32)

    features, cot_rows = (
        lax.all_gather(tokens, "col", axis=1, tiled=True),
        lax.all_gather(cotangent, "col", axis=1, tiled=True),
    )

    def rebuild(got, masks, pos):
        flat_got = got.reshape((n_row * width, block, block))
        base = (pos * width)[:, None]
        where = jnp.where(masks > 0, base + slot_of(masks), base + zero_slot)
        dense = flat_got.at[where.reshape(-1)].get(mode="promise_in_bounds")
        dense = dense.reshape((n_row, nb, block, block))
        dense = from_blocks(dense, nr, nc)
        return dense.reshape((n_row * nr * block, nc * block))

    up_whole = rebuild(got_up, masks_up, rows_n)
    preact = jnp.dot(features, up_whole, preferred_element_type=jnp.float32)
    gelu_value, gelu_slope = gelu_parts(preact)
    activation = gelu_value.astype(jnp.bfloat16)

    def kept_blocks(partial, masks, dest):
        view = partial.astype(jnp.bfloat16).reshape((n_row * nr, block, nc, block))
        idx = kept_index(masks, slots)
        rows = (dest * nr)[:, None] + idx // nc
        cols = idx % nc
        return view.at[rows, :, cols, :].get(mode="promise_in_bounds")

    def unpack(summed, own):
        dense = summed.at[slot_of(own)].get(mode="promise_in_bounds")
        keep = own[:, None, None] > 0
        dense = jnp.where(keep, dense.astype(jnp.float32), jnp.zeros(dense.shape, jnp.float32))
        return from_blocks(dense, nr, nc)

    def reduce_kept(sent, own):
        return unpack(lax.psum_scatter(sent, "row", scatter_dimension=0, tiled=True)[0], own)

    sent_down = kept_blocks(token_product(cot_rows, activation), masks_down, rows_n)
    got_down, sent_down = lax.optimization_barrier((got_down, sent_down))
    summed_down = lax.psum_scatter(sent_down, "row", scatter_dimension=0, tiled=True)[0]

    down_whole = rebuild(got_down, masks_down, rows_n)
    act_grad = jnp.dot(cot_rows, down_whole, preferred_element_type=jnp.float32)
    pre_grad = (act_grad * gelu_slope).astype(jnp.bfloat16)
    partial_tokens = lax.dot_general(
        pre_grad, up_whole, (((1,), (1,)), ((), ())), preferred_element_type=jnp.float32
    )
    sent_up = kept_blocks(token_product(features, pre_grad), masks_up, rows_n)
    summed_down, sent_up = lax.optimization_barrier((summed_down, sent_up))
    grad_down = unpack(summed_down, flat_down)
    grad_up = reduce_kept(sent_up, flat_up)

    token_grad = lax.psum_scatter(
        partial_tokens.astype(jnp.bfloat16), "col", scatter_dimension=1, tiled=True
    )
    new_up, new_moment_up, new_second_up = adam_update(w_up, moment_up, second_up, grad_up)
    new_down, new_moment_down, new_second_down = adam_update(
        w_down, moment_down, second_down, grad_down
    )
    return (
        token_grad,
        new_up,
        new_moment_up,
        new_second_up,
        new_down,
        new_moment_down,
        new_second_down,
    )


def solution(mesh):
    spec = P("row", "col")
    return jax.shard_map(
        shards,
        mesh=mesh,
        in_specs=(spec,) * 10,
        out_specs=(spec,) * 7,
        check_vma=False,
    )
```

```python
import functools

import jax
import jax.numpy as jnp
from jax import lax
from jax.sharding import PartitionSpec as P

inv_root_two = 0.7071067811865476
inv_root_two_pi = 0.3989422804014327
learn_rate = 0.001
bias_first = 1.0 - 0.9**10
bias_second = 1.0 - 0.95**10


def expand_mask(mask, block):
    blocks_r, blocks_c = mask.shape
    values = mask.astype(jnp.float32)[:, None, :, None]
    values = jnp.broadcast_to(values, (blocks_r, block, blocks_c, block))
    return values.reshape(blocks_r * block, blocks_c * block)


def gelu_parts(preact):
    normal_cdf = 0.5 * (1.0 + lax.erf(preact * inv_root_two))
    density = jnp.exp(-0.5 * preact * preact) * inv_root_two_pi
    return (preact * normal_cdf, normal_cdf + preact * density)


def adam_update(weight, moment, second, grad):
    moment_new = 0.9 * moment + 0.1 * grad
    second_new = 0.95 * second + 0.05 * grad * grad
    step_size = moment_new / bias_first / (jnp.sqrt(second_new / bias_second) + 1e-08)
    return (weight - learn_rate * step_size, moment_new, second_new)


def token_product(rows_full, other):
    return lax.dot_general(
        rows_full, other, (((0,), (0,)), ((), ())), preferred_element_type=jnp.float32
    )


def to_blocks(dense, block):
    rows, cols = dense.shape[-2:]
    lead = dense.shape[:-2]
    nr, nc = rows // block, cols // block
    x = dense.reshape(lead + (nr, block, nc, block))
    k = len(lead)
    x = jnp.moveaxis(x, k + 2, k + 1)
    return x.reshape(lead + (nr * nc, block, block))


def from_blocks(blocks, nr, nc):
    lead = blocks.shape[:-3]
    block = blocks.shape[-1]
    x = blocks.reshape(lead + (nr, nc, block, block))
    k = len(lead)
    x = jnp.moveaxis(x, k + 1, k + 2)
    return x.reshape(lead + (nr * block, nc * block))


def kept_index(flat_mask, slots):
    n = flat_mask.shape[-1]
    upto = jnp.cumsum(flat_mask, axis=-1)
    k = jnp.arange(slots, dtype=jnp.int32)
    idx = jnp.sum((upto[..., None, :] <= k[:, None]).astype(jnp.int32), axis=-1)
    return jnp.minimum(idx, n - 1)


def slot_of(flat_mask):
    return jnp.cumsum(flat_mask, axis=-1) - flat_mask


def row_ring(mesh):
    devices = mesh.devices
    n = devices.shape[0]
    try:
        pts = [tuple(devices[r, 0].coords) for r in range(n)]
    except AttributeError:
        return list(range(n))

    def near(a, b):
        return sum(abs(i - j) for i, j in zip(pts[a], pts[b])) == 1

    path, used, budget = [0], {0}, [20000]

    def search():
        budget[0] -= 1
        if budget[0] < 0:
            return False
        if len(path) == n:
            return near(path[-1], 0)
        options = [j for j in range(n) if j not in used and near(path[-1], j)]
        options.sort(key=lambda j: sum(1 for k in range(n) if k not in used and near(j, k)))
        for j in options:
            path.append(j)
            used.add(j)
            if search():
                return True
            path.pop()
            used.discard(j)
        return False

    if n > 2 and search():
        return path
    return list(range(n))


def shards(
    ring,
    tokens,
    cotangent,
    w_up,
    w_down,
    mask_up,
    mask_down,
    moment_up,
    second_up,
    moment_down,
    second_down,
):
    nr, nc = mask_up.shape
    nb = nr * nc
    block = w_up.shape[0] // nr
    slots = nb // 2
    n_row = lax.axis_size("row")
    width = slots + 2
    width += width % 2
    zero_slot = slots
    mask_slot = slots + 1
    half = width // 2
    rows_n = jnp.arange(n_row, dtype=jnp.int32)

    place = [0] * n_row
    for i, r in enumerate(ring):
        place[r] = i
    right = [(ring[i], ring[(i + 1) % n_row]) for i in range(n_row)]
    left = [(ring[i], ring[(i - 1) % n_row]) for i in range(n_row)]
    me = lax.axis_index("row")
    place_of = jnp.array(place, jnp.int32)
    ring_of = jnp.array(ring, jnp.int32)
    p = place_of[me]

    flat_up = mask_up.reshape(nb)
    flat_down = mask_down.reshape(nb)

    def package(w, flat):
        blocks = to_blocks(w.astype(jnp.bfloat16), block)
        kept = blocks.at[kept_index(flat, slots)].get(mode="promise_in_bounds")
        extra = jnp.zeros((width - slots, block, block), jnp.bfloat16)
        extra = extra.at[mask_slot - slots, 0, :nb].set(flat_up.astype(jnp.bfloat16))
        extra = extra.at[mask_slot - slots, 1, :nb].set(flat_down.astype(jnp.bfloat16))
        return jnp.concatenate([kept, extra], axis=0)

    def ring_gather(pk):
        a, b = pk[:half], pk[half:]
        got_a, got_b = [a], [b]
        for _ in range(1, n_row):
            a = lax.ppermute(a, "row", right)
            b = lax.ppermute(b, "row", left)
            got_a.append(a)
            got_b.append(b)
        return jnp.concatenate(
            [jnp.stack(got_a).reshape((n_row * half, block, block)),
             jnp.stack(got_b).reshape((n_row * half, block, block))],
            axis=0,
        )

    q = place_of
    step_a = (p - q) % n_row
    step_b = (q - p) % n_row

    def where_is(k):
        in_a = k < half
        return jnp.where(
            in_a,
            step_a[:, None] * half + k,
            n_row * half + step_b[:, None] * half + (k - half),
        )

    got_up = ring_gather(package(w_up, flat_up))
    got_down = ring_gather(package(w_down, flat_down))
    mask_blocks = got_up.at[where_is(jnp.full((n_row, 1), mask_slot, jnp.int32))[:, 0]].get(
        mode="promise_in_bounds"
    )
    masks_up = mask_blocks[:, 0, :nb].astype(jnp.int32)
    masks_down = mask_blocks[:, 1, :nb].astype(jnp.int32)

    features, cot_rows = (
        lax.all_gather(tokens, "col", axis=1, tiled=True),
        lax.all_gather(cotangent, "col", axis=1, tiled=True),
    )

    def rebuild(got, masks):
        k = jnp.where(masks > 0, slot_of(masks), zero_slot)
        dense = got.at[where_is(k).reshape(-1)].get(mode="promise_in_bounds")
        dense = dense.reshape((n_row, nb, block, block))
        dense = from_blocks(dense, nr, nc)
        return dense.reshape((n_row * nr * block, nc * block))

    def kept_blocks(partial, masks, dest, lo, hi):
        view = partial.astype(jnp.bfloat16).reshape((n_row * nr, block, nc, block))
        idx = kept_index(masks[dest], slots)[:, lo:hi]
        rows = (dest * nr)[:, None] + idx // nc
        cols = idx % nc
        return view.at[rows, :, cols, :].get(mode="promise_in_bounds")

    def ring_reduce(partial, masks):
        ha = (slots + 1) // 2
        dest_a = ring_of[(p - rows_n) % n_row]
        dest_b = ring_of[(p + rows_n) % n_row]
        sent_a = kept_blocks(partial, masks, dest_a, 0, ha)
        sent_b = kept_blocks(partial, masks, dest_b, ha, slots)
        acc_a, acc_b = sent_a[1], sent_b[1]
        for s in range(1, n_row):
            in_a = lax.ppermute(acc_a, "row", right).astype(jnp.float32)
            in_b = lax.ppermute(acc_b, "row", left).astype(jnp.float32)
            if s < n_row - 1:
                acc_a = (in_a + sent_a[s + 1].astype(jnp.float32)).astype(jnp.bfloat16)
                acc_b = (in_b + sent_b[s + 1].astype(jnp.float32)).astype(jnp.bfloat16)
        total_a = in_a + sent_a[0].astype(jnp.float32)
        total_b = in_b + sent_b[0].astype(jnp.float32)
        return jnp.concatenate([total_a, total_b], axis=0)

    def unpack(summed, own):
        dense = summed.at[slot_of(own)].get(mode="promise_in_bounds")
        keep = own[:, None, None] > 0
        dense = jnp.where(keep, dense, jnp.zeros(dense.shape, jnp.float32))
        return from_blocks(dense, nr, nc)

    up_whole = rebuild(got_up, masks_up)
    preact = jnp.dot(features, up_whole, preferred_element_type=jnp.float32)
    gelu_value, gelu_slope = gelu_parts(preact)
    activation = gelu_value.astype(jnp.bfloat16)
    grad_down = unpack(ring_reduce(token_product(cot_rows, activation), masks_down), flat_down)

    down_whole = rebuild(got_down, masks_down)
    act_grad = jnp.dot(cot_rows, down_whole, preferred_element_type=jnp.float32)
    pre_grad = (act_grad * gelu_slope).astype(jnp.bfloat16)
    partial_tokens = lax.dot_general(
        pre_grad, up_whole, (((1,), (1,)), ((), ())), preferred_element_type=jnp.float32
    )
    grad_up = unpack(ring_reduce(token_product(features, pre_grad), masks_up), flat_up)

    token_grad = lax.psum_scatter(
        partial_tokens.astype(jnp.bfloat16), "col", scatter_dimension=1, tiled=True
    )
    new_up, new_moment_up, new_second_up = adam_update(w_up, moment_up, second_up, grad_up)
    new_down, new_moment_down, new_second_down = adam_update(
        w_down, moment_down, second_down, grad_down
    )
    return (
        token_grad,
        new_up,
        new_moment_up,
        new_second_up,
        new_down,
        new_moment_down,
        new_second_down,
    )


def solution(mesh):
    spec = P("row", "col")
    return jax.shard_map(
        functools.partial(shards, row_ring(mesh)),
        mesh=mesh,
        in_specs=(spec,) * 10,
        out_specs=(spec,) * 7,
        check_vma=False,
    )
```

```python
import functools

import jax
import jax.numpy as jnp
from jax import lax
from jax.sharding import PartitionSpec as P

inv_root_two = 0.7071067811865476
inv_root_two_pi = 0.3989422804014327
learn_rate = 0.001
bias_first = 1.0 - 0.9**10
bias_second = 1.0 - 0.95**10


def expand_mask(mask, block):
    blocks_r, blocks_c = mask.shape
    values = mask.astype(jnp.float32)[:, None, :, None]
    values = jnp.broadcast_to(values, (blocks_r, block, blocks_c, block))
    return values.reshape(blocks_r * block, blocks_c * block)


def gelu_parts(preact):
    normal_cdf = 0.5 * (1.0 + lax.erf(preact * inv_root_two))
    density = jnp.exp(-0.5 * preact * preact) * inv_root_two_pi
    return (preact * normal_cdf, normal_cdf + preact * density)


def adam_update(weight, moment, second, grad):
    moment_new = 0.9 * moment + 0.1 * grad
    second_new = 0.95 * second + 0.05 * grad * grad
    step_size = moment_new / bias_first / (jnp.sqrt(second_new / bias_second) + 1e-08)
    return (weight - learn_rate * step_size, moment_new, second_new)


def token_product(rows_full, other):
    return lax.dot_general(
        rows_full, other, (((0,), (0,)), ((), ())), preferred_element_type=jnp.float32
    )


def to_blocks(dense, block):
    rows, cols = dense.shape[-2:]
    lead = dense.shape[:-2]
    nr, nc = rows // block, cols // block
    x = dense.reshape(lead + (nr, block, nc, block))
    k = len(lead)
    x = jnp.moveaxis(x, k + 2, k + 1)
    return x.reshape(lead + (nr * nc, block, block))


def from_blocks(blocks, nr, nc):
    lead = blocks.shape[:-3]
    block = blocks.shape[-1]
    x = blocks.reshape(lead + (nr, nc, block, block))
    k = len(lead)
    x = jnp.moveaxis(x, k + 1, k + 2)
    return x.reshape(lead + (nr * block, nc * block))


def kept_index(flat_mask, slots):
    n = flat_mask.shape[-1]
    upto = jnp.cumsum(flat_mask, axis=-1)
    k = jnp.arange(slots, dtype=jnp.int32)
    idx = jnp.sum((upto[..., None, :] <= k[:, None]).astype(jnp.int32), axis=-1)
    return jnp.minimum(idx, n - 1)


def slot_of(flat_mask):
    return jnp.cumsum(flat_mask, axis=-1) - flat_mask


def row_ring(mesh):
    devices = mesh.devices
    n = devices.shape[0]
    try:
        pts = [tuple(devices[r, 0].coords) for r in range(n)]
    except AttributeError:
        return list(range(n))

    def near(a, b):
        return sum(abs(i - j) for i, j in zip(pts[a], pts[b])) == 1

    path, used, budget = [0], {0}, [20000]

    def search():
        budget[0] -= 1
        if budget[0] < 0:
            return False
        if len(path) == n:
            return near(path[-1], 0)
        options = [j for j in range(n) if j not in used and near(path[-1], j)]
        options.sort(key=lambda j: sum(1 for k in range(n) if k not in used and near(j, k)))
        for j in options:
            path.append(j)
            used.add(j)
            if search():
                return True
            path.pop()
            used.discard(j)
        return False

    if n > 2 and search():
        return path
    return list(range(n))


def shards(
    ring,
    tokens,
    cotangent,
    w_up,
    w_down,
    mask_up,
    mask_down,
    moment_up,
    second_up,
    moment_down,
    second_down,
):
    nr, nc = mask_up.shape
    nb = nr * nc
    block = w_up.shape[0] // nr
    slots = nb // 2
    n_row = lax.axis_size("row")
    width = slots + 2
    width += width % 2
    zero_slot = slots
    mask_slot = slots + 1
    half = width // 2
    rows_n = jnp.arange(n_row, dtype=jnp.int32)

    place = [0] * n_row
    for i, r in enumerate(ring):
        place[r] = i
    right = [(ring[i], ring[(i + 1) % n_row]) for i in range(n_row)]
    left = [(ring[i], ring[(i - 1) % n_row]) for i in range(n_row)]
    me = lax.axis_index("row")
    place_of = jnp.array(place, jnp.int32)
    ring_of = jnp.array(ring, jnp.int32)
    p = place_of[me]

    flat_up = mask_up.reshape(nb)
    flat_down = mask_down.reshape(nb)

    def package(w, flat):
        blocks = to_blocks(w.astype(jnp.bfloat16), block)
        kept = blocks.at[kept_index(flat, slots)].get(mode="promise_in_bounds")
        extra = jnp.zeros((width - slots, block, block), jnp.bfloat16)
        extra = extra.at[mask_slot - slots, 0, :nb].set(flat_up.astype(jnp.bfloat16))
        extra = extra.at[mask_slot - slots, 1, :nb].set(flat_down.astype(jnp.bfloat16))
        return jnp.concatenate([kept, extra], axis=0)

    def ring_gather(pk):
        a, b = pk[:half], pk[half:]
        got_a, got_b = [a], [b]
        for _ in range(1, n_row):
            a = lax.ppermute(a, "row", right)
            b = lax.ppermute(b, "row", left)
            got_a.append(a)
            got_b.append(b)
        return jnp.concatenate(
            [jnp.stack(got_a).reshape((n_row * half, block, block)),
             jnp.stack(got_b).reshape((n_row * half, block, block))],
            axis=0,
        )

    q = place_of
    step_a = (p - q) % n_row
    step_b = (q - p) % n_row

    def where_is(k):
        in_a = k < half
        return jnp.where(
            in_a,
            step_a[:, None] * half + k,
            n_row * half + step_b[:, None] * half + (k - half),
        )

    got_up = ring_gather(package(w_up, flat_up))
    got_down = lax.all_gather(package(w_down, flat_down), "row", axis=0)
    mask_blocks = got_up.at[where_is(jnp.full((n_row, 1), mask_slot, jnp.int32))[:, 0]].get(
        mode="promise_in_bounds"
    )
    masks_up = mask_blocks[:, 0, :nb].astype(jnp.int32)
    masks_down = mask_blocks[:, 1, :nb].astype(jnp.int32)

    features, cot_rows = (
        lax.all_gather(tokens, "col", axis=1, tiled=True),
        lax.all_gather(cotangent, "col", axis=1, tiled=True),
    )

    def rebuild(got, masks, at):
        k = jnp.where(masks > 0, slot_of(masks), zero_slot)
        dense = got.at[at(k).reshape(-1)].get(mode="promise_in_bounds")
        dense = dense.reshape((n_row, nb, block, block))
        dense = from_blocks(dense, nr, nc)
        return dense.reshape((n_row * nr * block, nc * block))

    def in_order(k):
        return (rows_n * width)[:, None] + k

    def kept_blocks(partial, masks, dest, lo, hi):
        view = partial.astype(jnp.bfloat16).reshape((n_row * nr, block, nc, block))
        idx = kept_index(masks[dest], slots)[:, lo:hi]
        rows = (dest * nr)[:, None] + idx // nc
        cols = idx % nc
        return view.at[rows, :, cols, :].get(mode="promise_in_bounds")

    def ring_reduce(partial, masks, hold=None):
        ha = (slots + 1) // 2
        dest_a = ring_of[(p - rows_n) % n_row]
        dest_b = ring_of[(p + rows_n) % n_row]
        sent_a = kept_blocks(partial, masks, dest_a, 0, ha)
        sent_b = kept_blocks(partial, masks, dest_b, ha, slots)
        if hold is not None:
            hold, sent_a, sent_b = lax.optimization_barrier((hold, sent_a, sent_b))
        acc_a, acc_b = sent_a[1], sent_b[1]
        for s in range(1, n_row):
            in_a = lax.ppermute(acc_a, "row", right).astype(jnp.float32)
            in_b = lax.ppermute(acc_b, "row", left).astype(jnp.float32)
            if s < n_row - 1:
                acc_a = (in_a + sent_a[s + 1].astype(jnp.float32)).astype(jnp.bfloat16)
                acc_b = (in_b + sent_b[s + 1].astype(jnp.float32)).astype(jnp.bfloat16)
        total_a = in_a + sent_a[0].astype(jnp.float32)
        total_b = in_b + sent_b[0].astype(jnp.float32)
        return jnp.concatenate([total_a, total_b], axis=0), hold

    def unpack(summed, own):
        dense = summed.at[slot_of(own)].get(mode="promise_in_bounds")
        keep = own[:, None, None] > 0
        dense = jnp.where(keep, dense, jnp.zeros(dense.shape, jnp.float32))
        return from_blocks(dense, nr, nc)

    up_whole = rebuild(got_up, masks_up, where_is)
    preact = jnp.dot(features, up_whole, preferred_element_type=jnp.float32)
    gelu_value, gelu_slope = gelu_parts(preact)
    activation = gelu_value.astype(jnp.bfloat16)
    sent_down = kept_blocks(token_product(cot_rows, activation), masks_down, rows_n, 0, slots)
    got_down, sent_down = lax.optimization_barrier((got_down, sent_down))
    summed_down = lax.psum_scatter(sent_down, "row", scatter_dimension=0, tiled=True)[0]

    down_whole = rebuild(got_down.reshape((n_row * width, block, block)), masks_down, in_order)
    act_grad = jnp.dot(cot_rows, down_whole, preferred_element_type=jnp.float32)
    pre_grad = (act_grad * gelu_slope).astype(jnp.bfloat16)
    partial_tokens = lax.dot_general(
        pre_grad, up_whole, (((1,), (1,)), ((), ())), preferred_element_type=jnp.float32
    )
    summed_up, summed_down = ring_reduce(token_product(features, pre_grad), masks_up, summed_down)
    grad_down = unpack(summed_down.astype(jnp.float32), flat_down)
    grad_up = unpack(summed_up, flat_up)

    token_grad = lax.psum_scatter(
        partial_tokens.astype(jnp.bfloat16), "col", scatter_dimension=1, tiled=True
    )
    new_up, new_moment_up, new_second_up = adam_update(w_up, moment_up, second_up, grad_up)
    new_down, new_moment_down, new_second_down = adam_update(
        w_down, moment_down, second_down, grad_down
    )
    return (
        token_grad,
        new_up,
        new_moment_up,
        new_second_up,
        new_down,
        new_moment_down,
        new_second_down,
    )


def solution(mesh):
    spec = P("row", "col")
    return jax.shard_map(
        functools.partial(shards, row_ring(mesh)),
        mesh=mesh,
        in_specs=(spec,) * 10,
        out_specs=(spec,) * 7,
        check_vma=False,
    )
```

```python
import functools

import jax
import jax.numpy as jnp
from jax import lax
from jax.sharding import PartitionSpec as P

inv_root_two = 0.7071067811865476
inv_root_two_pi = 0.3989422804014327
learn_rate = 0.001
bias_first = 1.0 - 0.9**10
bias_second = 1.0 - 0.95**10


def expand_mask(mask, block):
    blocks_r, blocks_c = mask.shape
    values = mask.astype(jnp.float32)[:, None, :, None]
    values = jnp.broadcast_to(values, (blocks_r, block, blocks_c, block))
    return values.reshape(blocks_r * block, blocks_c * block)


def gelu_parts(preact):
    normal_cdf = 0.5 * (1.0 + lax.erf(preact * inv_root_two))
    density = jnp.exp(-0.5 * preact * preact) * inv_root_two_pi
    return (preact * normal_cdf, normal_cdf + preact * density)


def adam_update(weight, moment, second, grad):
    moment_new = 0.9 * moment + 0.1 * grad
    second_new = 0.95 * second + 0.05 * grad * grad
    step_size = moment_new / bias_first / (jnp.sqrt(second_new / bias_second) + 1e-08)
    return (weight - learn_rate * step_size, moment_new, second_new)


def token_product(rows_full, other):
    return lax.dot_general(
        rows_full, other, (((0,), (0,)), ((), ())), preferred_element_type=jnp.float32
    )


def to_blocks(dense, block):
    rows, cols = dense.shape[-2:]
    lead = dense.shape[:-2]
    nr, nc = rows // block, cols // block
    x = dense.reshape(lead + (nr, block, nc, block))
    k = len(lead)
    x = jnp.moveaxis(x, k + 2, k + 1)
    return x.reshape(lead + (nr * nc, block, block))


def from_blocks(blocks, nr, nc):
    lead = blocks.shape[:-3]
    block = blocks.shape[-1]
    x = blocks.reshape(lead + (nr, nc, block, block))
    k = len(lead)
    x = jnp.moveaxis(x, k + 1, k + 2)
    return x.reshape(lead + (nr * block, nc * block))


def kept_index(flat_mask, slots):
    n = flat_mask.shape[-1]
    upto = jnp.cumsum(flat_mask, axis=-1)
    k = jnp.arange(slots, dtype=jnp.int32)
    idx = jnp.sum((upto[..., None, :] <= k[:, None]).astype(jnp.int32), axis=-1)
    return jnp.minimum(idx, n - 1)


def slot_of(flat_mask):
    return jnp.cumsum(flat_mask, axis=-1) - flat_mask


def row_ring(mesh):
    devices = mesh.devices
    n = devices.shape[0]
    try:
        pts = [tuple(devices[r, 0].coords) for r in range(n)]
    except AttributeError:
        return list(range(n))

    def near(a, b):
        return sum(abs(i - j) for i, j in zip(pts[a], pts[b])) == 1

    path, used, budget = [0], {0}, [20000]

    def search():
        budget[0] -= 1
        if budget[0] < 0:
            return False
        if len(path) == n:
            return near(path[-1], 0)
        options = [j for j in range(n) if j not in used and near(path[-1], j)]
        options.sort(key=lambda j: sum(1 for k in range(n) if k not in used and near(j, k)))
        for j in options:
            path.append(j)
            used.add(j)
            if search():
                return True
            path.pop()
            used.discard(j)
        return False

    if n > 2 and search():
        return path
    return list(range(n))


def shards(
    ring,
    tokens,
    cotangent,
    w_up,
    w_down,
    mask_up,
    mask_down,
    moment_up,
    second_up,
    moment_down,
    second_down,
):
    nr, nc = mask_up.shape
    nb = nr * nc
    block = w_up.shape[0] // nr
    slots = nb // 2
    n_row = lax.axis_size("row")
    width = slots + 2
    width += width % 2
    zero_slot = slots
    mask_slot = slots + 1
    half = width // 2
    rows_n = jnp.arange(n_row, dtype=jnp.int32)

    place = [0] * n_row
    for i, r in enumerate(ring):
        place[r] = i
    right = [(ring[i], ring[(i + 1) % n_row]) for i in range(n_row)]
    left = [(ring[i], ring[(i - 1) % n_row]) for i in range(n_row)]
    me = lax.axis_index("row")
    place_of = jnp.array(place, jnp.int32)
    ring_of = jnp.array(ring, jnp.int32)
    p = place_of[me]

    flat_up = mask_up.reshape(nb)
    flat_down = mask_down.reshape(nb)

    def package(w, flat):
        blocks = to_blocks(w.astype(jnp.bfloat16), block)
        kept = blocks.at[kept_index(flat, slots)].get(mode="promise_in_bounds")
        extra = jnp.zeros((width - slots, block, block), jnp.bfloat16)
        extra = extra.at[mask_slot - slots, 0, :nb].set(flat_up.astype(jnp.bfloat16))
        extra = extra.at[mask_slot - slots, 1, :nb].set(flat_down.astype(jnp.bfloat16))
        return jnp.concatenate([kept, extra], axis=0)

    def ring_gather(pk):
        a, b = pk[:half], pk[half:]
        got_a, got_b = [a], [b]
        for _ in range(1, n_row):
            a = lax.ppermute(a, "row", right)
            b = lax.ppermute(b, "row", left)
            got_a.append(a)
            got_b.append(b)
        return jnp.concatenate(
            [jnp.stack(got_a).reshape((n_row * half, block, block)),
             jnp.stack(got_b).reshape((n_row * half, block, block))],
            axis=0,
        )

    q = place_of
    step_a = (p - q) % n_row
    step_b = (q - p) % n_row

    def where_is(k):
        in_a = k < half
        return jnp.where(
            in_a,
            step_a[:, None] * half + k,
            n_row * half + step_b[:, None] * half + (k - half),
        )

    got_up = ring_gather(package(w_up, flat_up))
    got_down = lax.all_gather(package(w_down, flat_down), "row", axis=0)
    mask_blocks = got_up.at[where_is(jnp.full((n_row, 1), mask_slot, jnp.int32))[:, 0]].get(
        mode="promise_in_bounds"
    )
    masks_up = mask_blocks[:, 0, :nb].astype(jnp.int32)
    masks_down = mask_blocks[:, 1, :nb].astype(jnp.int32)

    features, cot_rows = (
        lax.all_gather(tokens, "col", axis=1, tiled=True),
        lax.all_gather(cotangent, "col", axis=1, tiled=True),
    )

    def rebuild(got, masks, at):
        k = jnp.where(masks > 0, slot_of(masks), zero_slot)
        dense = got.at[at(k).reshape(-1)].get(mode="promise_in_bounds")
        return dense.reshape((n_row * nr, nc, block, block))

    def in_order(k):
        return (rows_n * width)[:, None] + k

    def kept_blocks(partial, masks, dest, lo, hi):
        view = partial.astype(jnp.bfloat16).reshape((n_row * nr, block, nc, block))
        idx = kept_index(masks[dest], slots)[:, lo:hi]
        rows = (dest * nr)[:, None] + idx // nc
        cols = idx % nc
        return view.at[rows, :, cols, :].get(mode="promise_in_bounds")

    def ring_reduce(partial, masks, hold=None):
        ha = (slots + 1) // 2
        dest_a = ring_of[(p - rows_n) % n_row]
        dest_b = ring_of[(p + rows_n) % n_row]
        sent_a = kept_blocks(partial, masks, dest_a, 0, ha)
        sent_b = kept_blocks(partial, masks, dest_b, ha, slots)
        if hold is not None:
            hold, sent_a, sent_b = lax.optimization_barrier((hold, sent_a, sent_b))
        acc_a, acc_b = sent_a[1], sent_b[1]
        for s in range(1, n_row):
            in_a = lax.ppermute(acc_a, "row", right).astype(jnp.float32)
            in_b = lax.ppermute(acc_b, "row", left).astype(jnp.float32)
            if s < n_row - 1:
                acc_a = (in_a + sent_a[s + 1].astype(jnp.float32)).astype(jnp.bfloat16)
                acc_b = (in_b + sent_b[s + 1].astype(jnp.float32)).astype(jnp.bfloat16)
        total_a = in_a + sent_a[0].astype(jnp.float32)
        total_b = in_b + sent_b[0].astype(jnp.float32)
        return jnp.concatenate([total_a, total_b], axis=0), hold

    def unpack(summed, own):
        dense = summed.at[slot_of(own)].get(mode="promise_in_bounds")
        keep = own[:, None, None] > 0
        dense = jnp.where(keep, dense, jnp.zeros(dense.shape, jnp.float32))
        return from_blocks(dense, nr, nc)

    up_whole = rebuild(got_up, masks_up, where_is)
    features3 = features.reshape((features.shape[0], n_row * nr, block))
    cot3 = cot_rows.reshape((cot_rows.shape[0], n_row * nr, block))

    def forward(rows3, w4):
        out = lax.dot_general(
            rows3, w4, (((1, 2), (0, 2)), ((), ())), preferred_element_type=jnp.float32
        )
        return out.reshape((out.shape[0], nc * block))

    def grad_view(rows3, acts):
        acts3 = acts.reshape((acts.shape[0], nc, block))
        out = lax.dot_general(
            rows3, acts3, (((0,), (0,)), ((), ())), preferred_element_type=jnp.float32
        )
        return out.reshape((n_row * nr * block, nc * block))

    preact = forward(features3, up_whole)
    gelu_value, gelu_slope = gelu_parts(preact)
    activation = gelu_value.astype(jnp.bfloat16)
    sent_down = kept_blocks(grad_view(cot3, activation), masks_down, rows_n, 0, slots)
    got_down, sent_down = lax.optimization_barrier((got_down, sent_down))
    summed_down = lax.psum_scatter(sent_down, "row", scatter_dimension=0, tiled=True)[0]

    down_whole = rebuild(got_down.reshape((n_row * width, block, block)), masks_down, in_order)
    act_grad = forward(cot3, down_whole)
    pre_grad = (act_grad * gelu_slope).astype(jnp.bfloat16)
    partial_tokens = lax.dot_general(
        pre_grad.reshape((pre_grad.shape[0], nc, block)),
        up_whole,
        (((1, 2), (1, 3)), ((), ())),
        preferred_element_type=jnp.float32,
    ).reshape((pre_grad.shape[0], n_row * nr * block))
    summed_up, summed_down = ring_reduce(grad_view(features3, pre_grad), masks_up, summed_down)
    grad_down = unpack(summed_down.astype(jnp.float32), flat_down)
    grad_up = unpack(summed_up, flat_up)

    token_grad = lax.psum_scatter(
        partial_tokens.astype(jnp.bfloat16), "col", scatter_dimension=1, tiled=True
    )
    new_up, new_moment_up, new_second_up = adam_update(w_up, moment_up, second_up, grad_up)
    new_down, new_moment_down, new_second_down = adam_update(
        w_down, moment_down, second_down, grad_down
    )
    return (
        token_grad,
        new_up,
        new_moment_up,
        new_second_up,
        new_down,
        new_moment_down,
        new_second_down,
    )


def solution(mesh):
    spec = P("row", "col")
    return jax.shard_map(
        functools.partial(shards, row_ring(mesh)),
        mesh=mesh,
        in_specs=(spec,) * 10,
        out_specs=(spec,) * 7,
        check_vma=False,
    )
```

```python
import functools

import jax
import jax.numpy as jnp
from jax import lax
from jax.sharding import PartitionSpec as P

inv_root_two = 0.7071067811865476
inv_root_two_pi = 0.3989422804014327
learn_rate = 0.001
bias_first = 1.0 - 0.9**10
bias_second = 1.0 - 0.95**10


def expand_mask(mask, block):
    blocks_r, blocks_c = mask.shape
    values = mask.astype(jnp.float32)[:, None, :, None]
    values = jnp.broadcast_to(values, (blocks_r, block, blocks_c, block))
    return values.reshape(blocks_r * block, blocks_c * block)


def gelu_parts(preact):
    normal_cdf = 0.5 * (1.0 + lax.erf(preact * inv_root_two))
    density = jnp.exp(-0.5 * preact * preact) * inv_root_two_pi
    return (preact * normal_cdf, normal_cdf + preact * density)


def adam_update(weight, moment, second, grad):
    moment_new = 0.9 * moment + 0.1 * grad
    second_new = 0.95 * second + 0.05 * grad * grad
    step_size = moment_new / bias_first / (jnp.sqrt(second_new / bias_second) + 1e-08)
    return (weight - learn_rate * step_size, moment_new, second_new)


def token_product(rows_full, other):
    return lax.dot_general(
        rows_full, other, (((0,), (0,)), ((), ())), preferred_element_type=jnp.float32
    )


def to_blocks(dense, block):
    rows, cols = dense.shape[-2:]
    lead = dense.shape[:-2]
    nr, nc = rows // block, cols // block
    x = dense.reshape(lead + (nr, block, nc, block))
    k = len(lead)
    x = jnp.moveaxis(x, k + 2, k + 1)
    return x.reshape(lead + (nr * nc, block, block))


def from_blocks(blocks, nr, nc):
    lead = blocks.shape[:-3]
    block = blocks.shape[-1]
    x = blocks.reshape(lead + (nr, nc, block, block))
    k = len(lead)
    x = jnp.moveaxis(x, k + 1, k + 2)
    return x.reshape(lead + (nr * block, nc * block))


def kept_index(flat_mask, slots):
    n = flat_mask.shape[-1]
    upto = jnp.cumsum(flat_mask, axis=-1)
    k = jnp.arange(slots, dtype=jnp.int32)
    idx = jnp.sum((upto[..., None, :] <= k[:, None]).astype(jnp.int32), axis=-1)
    return jnp.minimum(idx, n - 1)


def slot_of(flat_mask):
    return jnp.cumsum(flat_mask, axis=-1) - flat_mask


def row_ring(mesh):
    devices = mesh.devices
    n = devices.shape[0]
    try:
        pts = [tuple(devices[r, 0].coords) for r in range(n)]
    except AttributeError:
        return list(range(n))

    def near(a, b):
        return sum(abs(i - j) for i, j in zip(pts[a], pts[b])) == 1

    path, used, budget = [0], {0}, [20000]

    def search():
        budget[0] -= 1
        if budget[0] < 0:
            return False
        if len(path) == n:
            return near(path[-1], 0)
        options = [j for j in range(n) if j not in used and near(path[-1], j)]
        options.sort(key=lambda j: sum(1 for k in range(n) if k not in used and near(j, k)))
        for j in options:
            path.append(j)
            used.add(j)
            if search():
                return True
            path.pop()
            used.discard(j)
        return False

    if n > 2 and search():
        return path
    return list(range(n))


def shards(
    ring,
    tokens,
    cotangent,
    w_up,
    w_down,
    mask_up,
    mask_down,
    moment_up,
    second_up,
    moment_down,
    second_down,
):
    nr, nc = mask_up.shape
    nb = nr * nc
    block = w_up.shape[0] // nr
    slots = nb // 2
    n_row = lax.axis_size("row")
    width = slots + 2
    width += width % 2
    zero_slot = slots
    mask_slot = slots + 1
    half = width // 2
    rows_n = jnp.arange(n_row, dtype=jnp.int32)

    place = [0] * n_row
    for i, r in enumerate(ring):
        place[r] = i
    right = [(ring[i], ring[(i + 1) % n_row]) for i in range(n_row)]
    left = [(ring[i], ring[(i - 1) % n_row]) for i in range(n_row)]
    me = lax.axis_index("row")
    place_of = jnp.array(place, jnp.int32)
    ring_of = jnp.array(ring, jnp.int32)
    p = place_of[me]

    flat_up = mask_up.reshape(nb)
    flat_down = mask_down.reshape(nb)

    def package(w, flat):
        blocks = to_blocks(w.astype(jnp.bfloat16), block)
        kept = blocks.at[kept_index(flat, slots)].get(mode="promise_in_bounds")
        extra = jnp.zeros((width - slots, block, block), jnp.bfloat16)
        extra = extra.at[mask_slot - slots, 0, :nb].set(flat_up.astype(jnp.bfloat16))
        extra = extra.at[mask_slot - slots, 1, :nb].set(flat_down.astype(jnp.bfloat16))
        return jnp.concatenate([kept, extra], axis=0)

    def ring_gather(pk):
        a, b = pk[:half], pk[half:]
        got_a, got_b = [a], [b]
        for _ in range(1, n_row):
            a = lax.ppermute(a, "row", right)
            b = lax.ppermute(b, "row", left)
            got_a.append(a)
            got_b.append(b)
        return jnp.concatenate(
            [jnp.stack(got_a).reshape((n_row * half, block, block)),
             jnp.stack(got_b).reshape((n_row * half, block, block))],
            axis=0,
        )

    q = place_of
    step_a = (p - q) % n_row
    step_b = (q - p) % n_row

    def where_is(k):
        in_a = k < half
        return jnp.where(
            in_a,
            step_a[:, None] * half + k,
            n_row * half + step_b[:, None] * half + (k - half),
        )

    got_up = ring_gather(package(w_up, flat_up))
    got_up, package_down = lax.optimization_barrier((got_up, package(w_down, flat_down)))
    got_down = lax.all_gather(package_down, "row", axis=0)
    mask_blocks = got_up.at[where_is(jnp.full((n_row, 1), mask_slot, jnp.int32))[:, 0]].get(
        mode="promise_in_bounds"
    )
    masks_up = mask_blocks[:, 0, :nb].astype(jnp.int32)
    masks_down = mask_blocks[:, 1, :nb].astype(jnp.int32)

    features, cot_rows = (
        lax.all_gather(tokens, "col", axis=1, tiled=True),
        lax.all_gather(cotangent, "col", axis=1, tiled=True),
    )

    def rebuild(got, masks, at):
        k = jnp.where(masks > 0, slot_of(masks), zero_slot)
        dense = got.at[at(k).reshape(-1)].get(mode="promise_in_bounds")
        return dense.reshape((n_row * nr, nc, block, block))

    def in_order(k):
        return (rows_n * width)[:, None] + k

    def kept_blocks(partial, masks, dest, lo, hi):
        view = partial.astype(jnp.bfloat16).reshape((n_row * nr, block, nc, block))
        idx = kept_index(masks[dest], slots)[:, lo:hi]
        rows = (dest * nr)[:, None] + idx // nc
        cols = idx % nc
        return view.at[rows, :, cols, :].get(mode="promise_in_bounds")

    def ring_reduce(partial, masks, hold=None):
        ha = (slots + 1) // 2
        dest_a = ring_of[(p - rows_n) % n_row]
        dest_b = ring_of[(p + rows_n) % n_row]
        sent_a = kept_blocks(partial, masks, dest_a, 0, ha)
        sent_b = kept_blocks(partial, masks, dest_b, ha, slots)
        if hold is not None:
            hold, sent_a, sent_b = lax.optimization_barrier((hold, sent_a, sent_b))
        acc_a, acc_b = sent_a[1], sent_b[1]
        for s in range(1, n_row):
            in_a = lax.ppermute(acc_a, "row", right).astype(jnp.float32)
            in_b = lax.ppermute(acc_b, "row", left).astype(jnp.float32)
            if s < n_row - 1:
                acc_a = (in_a + sent_a[s + 1].astype(jnp.float32)).astype(jnp.bfloat16)
                acc_b = (in_b + sent_b[s + 1].astype(jnp.float32)).astype(jnp.bfloat16)
        total_a = in_a + sent_a[0].astype(jnp.float32)
        total_b = in_b + sent_b[0].astype(jnp.float32)
        return jnp.concatenate([total_a, total_b], axis=0), hold

    def unpack(summed, own):
        dense = summed.at[slot_of(own)].get(mode="promise_in_bounds")
        keep = own[:, None, None] > 0
        dense = jnp.where(keep, dense, jnp.zeros(dense.shape, jnp.float32))
        return from_blocks(dense, nr, nc)

    up_whole = rebuild(got_up, masks_up, where_is)
    features3 = features.reshape((features.shape[0], n_row * nr, block))
    cot3 = cot_rows.reshape((cot_rows.shape[0], n_row * nr, block))

    def forward(rows3, w4):
        out = lax.dot_general(
            rows3, w4, (((1, 2), (0, 2)), ((), ())), preferred_element_type=jnp.float32
        )
        return out.reshape((out.shape[0], nc * block))

    def grad_view(rows3, acts):
        acts3 = acts.reshape((acts.shape[0], nc, block))
        out = lax.dot_general(
            rows3, acts3, (((0,), (0,)), ((), ())), preferred_element_type=jnp.float32
        )
        return out.reshape((n_row * nr * block, nc * block))

    preact = forward(features3, up_whole)
    gelu_value, gelu_slope = gelu_parts(preact)
    activation = gelu_value.astype(jnp.bfloat16)
    sent_down = kept_blocks(grad_view(cot3, activation), masks_down, rows_n, 0, slots)
    got_down, sent_down = lax.optimization_barrier((got_down, sent_down))
    summed_down = lax.psum_scatter(sent_down, "row", scatter_dimension=0, tiled=True)[0]

    down_whole = rebuild(got_down.reshape((n_row * width, block, block)), masks_down, in_order)
    act_grad = forward(cot3, down_whole)
    pre_grad = (act_grad * gelu_slope).astype(jnp.bfloat16)
    partial_tokens = lax.dot_general(
        pre_grad.reshape((pre_grad.shape[0], nc, block)),
        up_whole,
        (((1, 2), (1, 3)), ((), ())),
        preferred_element_type=jnp.float32,
    ).reshape((pre_grad.shape[0], n_row * nr * block))
    summed_up, summed_down = ring_reduce(grad_view(features3, pre_grad), masks_up, summed_down)
    grad_down = unpack(summed_down.astype(jnp.float32), flat_down)
    grad_up = unpack(summed_up, flat_up)

    token_grad = lax.psum_scatter(
        partial_tokens.astype(jnp.bfloat16), "col", scatter_dimension=1, tiled=True
    )
    new_up, new_moment_up, new_second_up = adam_update(w_up, moment_up, second_up, grad_up)
    new_down, new_moment_down, new_second_down = adam_update(
        w_down, moment_down, second_down, grad_down
    )
    return (
        token_grad,
        new_up,
        new_moment_up,
        new_second_up,
        new_down,
        new_moment_down,
        new_second_down,
    )


def solution(mesh):
    spec = P("row", "col")
    return jax.shard_map(
        functools.partial(shards, row_ring(mesh)),
        mesh=mesh,
        in_specs=(spec,) * 10,
        out_specs=(spec,) * 7,
        check_vma=False,
    )
```

```python
import functools

import jax
import jax.numpy as jnp
from jax import lax
from jax.sharding import PartitionSpec as P

inv_root_two = 0.7071067811865476
inv_root_two_pi = 0.3989422804014327
learn_rate = 0.001
bias_first = 1.0 - 0.9**10
bias_second = 1.0 - 0.95**10


def expand_mask(mask, block):
    blocks_r, blocks_c = mask.shape
    values = mask.astype(jnp.float32)[:, None, :, None]
    values = jnp.broadcast_to(values, (blocks_r, block, blocks_c, block))
    return values.reshape(blocks_r * block, blocks_c * block)


def gelu_parts(preact):
    normal_cdf = 0.5 * (1.0 + lax.erf(preact * inv_root_two))
    density = jnp.exp(-0.5 * preact * preact) * inv_root_two_pi
    return (preact * normal_cdf, normal_cdf + preact * density)


def adam_update(weight, moment, second, grad):
    moment_new = 0.9 * moment + 0.1 * grad
    second_new = 0.95 * second + 0.05 * grad * grad
    step_size = moment_new / bias_first / (jnp.sqrt(second_new / bias_second) + 1e-08)
    return (weight - learn_rate * step_size, moment_new, second_new)


def token_product(rows_full, other):
    return lax.dot_general(
        rows_full, other, (((0,), (0,)), ((), ())), preferred_element_type=jnp.float32
    )


def to_blocks(dense, block):
    rows, cols = dense.shape[-2:]
    lead = dense.shape[:-2]
    nr, nc = rows // block, cols // block
    x = dense.reshape(lead + (nr, block, nc, block))
    k = len(lead)
    x = jnp.moveaxis(x, k + 2, k + 1)
    return x.reshape(lead + (nr * nc, block, block))


def from_blocks(blocks, nr, nc):
    lead = blocks.shape[:-3]
    block = blocks.shape[-1]
    x = blocks.reshape(lead + (nr, nc, block, block))
    k = len(lead)
    x = jnp.moveaxis(x, k + 1, k + 2)
    return x.reshape(lead + (nr * block, nc * block))


def kept_index(flat_mask, slots):
    n = flat_mask.shape[-1]
    upto = jnp.cumsum(flat_mask, axis=-1)
    k = jnp.arange(slots, dtype=jnp.int32)
    idx = jnp.sum((upto[..., None, :] <= k[:, None]).astype(jnp.int32), axis=-1)
    return jnp.minimum(idx, n - 1)


def slot_of(flat_mask):
    return jnp.cumsum(flat_mask, axis=-1) - flat_mask


def row_ring(mesh):
    devices = mesh.devices
    n = devices.shape[0]
    try:
        pts = [tuple(devices[r, 0].coords) for r in range(n)]
    except AttributeError:
        return list(range(n))

    def near(a, b):
        return sum(abs(i - j) for i, j in zip(pts[a], pts[b])) == 1

    path, used, budget = [0], {0}, [20000]

    def search():
        budget[0] -= 1
        if budget[0] < 0:
            return False
        if len(path) == n:
            return near(path[-1], 0)
        options = [j for j in range(n) if j not in used and near(path[-1], j)]
        options.sort(key=lambda j: sum(1 for k in range(n) if k not in used and near(j, k)))
        for j in options:
            path.append(j)
            used.add(j)
            if search():
                return True
            path.pop()
            used.discard(j)
        return False

    if n > 2 and search():
        return path
    return list(range(n))


def shards(
    ring,
    tokens,
    cotangent,
    w_up,
    w_down,
    mask_up,
    mask_down,
    moment_up,
    second_up,
    moment_down,
    second_down,
):
    nr, nc = mask_up.shape
    nb = nr * nc
    block = w_up.shape[0] // nr
    slots = nb // 2
    n_row = lax.axis_size("row")
    width = slots + 2
    width += width % 2
    zero_slot = slots
    mask_slot = slots + 1
    half = width // 2
    rows_n = jnp.arange(n_row, dtype=jnp.int32)

    place = [0] * n_row
    for i, r in enumerate(ring):
        place[r] = i
    right = [(ring[i], ring[(i + 1) % n_row]) for i in range(n_row)]
    left = [(ring[i], ring[(i - 1) % n_row]) for i in range(n_row)]
    me = lax.axis_index("row")
    place_of = jnp.array(place, jnp.int32)
    ring_of = jnp.array(ring, jnp.int32)
    p = place_of[me]

    flat_up = mask_up.reshape(nb)
    flat_down = mask_down.reshape(nb)

    def package(w, flat):
        blocks = to_blocks(w.astype(jnp.bfloat16), block)
        kept = blocks.at[kept_index(flat, slots)].get(mode="promise_in_bounds")
        extra = jnp.zeros((width - slots, block, block), jnp.bfloat16)
        extra = extra.at[mask_slot - slots, 0, :nb].set(flat_up.astype(jnp.bfloat16))
        extra = extra.at[mask_slot - slots, 1, :nb].set(flat_down.astype(jnp.bfloat16))
        return jnp.concatenate([kept, extra], axis=0)

    def ring_gather(pk):
        a, b = pk[:half], pk[half:]
        got_a, got_b = [a], [b]
        for _ in range(1, n_row):
            a = lax.ppermute(a, "row", right)
            b = lax.ppermute(b, "row", left)
            got_a.append(a)
            got_b.append(b)
        return jnp.concatenate(
            [jnp.stack(got_a).reshape((n_row * half, block, block)),
             jnp.stack(got_b).reshape((n_row * half, block, block))],
            axis=0,
        )

    q = place_of
    step_a = (p - q) % n_row
    step_b = (q - p) % n_row

    def where_is(k):
        in_a = k < half
        return jnp.where(
            in_a,
            step_a[:, None] * half + k,
            n_row * half + step_b[:, None] * half + (k - half),
        )

    got_up = ring_gather(package(w_up, flat_up))
    got_up, package_down = lax.optimization_barrier((got_up, package(w_down, flat_down)))
    got_down = lax.all_gather(package_down, "row", axis=0)
    mask_blocks = got_up.at[where_is(jnp.full((n_row, 1), mask_slot, jnp.int32))[:, 0]].get(
        mode="promise_in_bounds"
    )
    masks_up = mask_blocks[:, 0, :nb].astype(jnp.int32)
    masks_down = mask_blocks[:, 1, :nb].astype(jnp.int32)

    features, cot_rows = (
        lax.all_gather(tokens, "col", axis=1, tiled=True),
        lax.all_gather(cotangent, "col", axis=1, tiled=True),
    )

    def rebuild(got, masks, at):
        k = jnp.where(masks > 0, slot_of(masks), zero_slot)
        dense = got.at[at(k).reshape(-1)].get(mode="promise_in_bounds")
        return dense.reshape((n_row * nr, nc, block, block))

    def in_order(k):
        return (rows_n * width)[:, None] + k

    def kept_blocks(partial, masks, dest, lo, hi):
        view = partial.astype(jnp.bfloat16).reshape((n_row * nr, block, nc, block))
        idx = kept_index(masks[dest], slots)[:, lo:hi]
        rows = (dest * nr)[:, None] + idx // nc
        cols = idx % nc
        return view.at[rows, :, cols, :].get(mode="promise_in_bounds")

    def ring_reduce(partial, masks, hold=None):
        ha = (slots + 1) // 2
        dest_a = ring_of[(p - rows_n) % n_row]
        dest_b = ring_of[(p + rows_n) % n_row]
        sent_a = kept_blocks(partial, masks, dest_a, 0, ha)
        sent_b = kept_blocks(partial, masks, dest_b, ha, slots)
        if hold is not None:
            hold, sent_a, sent_b = lax.optimization_barrier((hold, sent_a, sent_b))
        acc_a, acc_b = sent_a[1], sent_b[1]
        for s in range(1, n_row):
            in_a = lax.ppermute(acc_a, "row", right).astype(jnp.float32)
            in_b = lax.ppermute(acc_b, "row", left).astype(jnp.float32)
            if s < n_row - 1:
                acc_a = (in_a + sent_a[s + 1].astype(jnp.float32)).astype(jnp.bfloat16)
                acc_b = (in_b + sent_b[s + 1].astype(jnp.float32)).astype(jnp.bfloat16)
        total_a = in_a + sent_a[0].astype(jnp.float32)
        total_b = in_b + sent_b[0].astype(jnp.float32)
        return jnp.concatenate([total_a, total_b], axis=0), hold

    def unpack(summed, own):
        dense = summed.at[slot_of(own)].get(mode="promise_in_bounds")
        keep = own[:, None, None] > 0
        dense = jnp.where(keep, dense, jnp.zeros(dense.shape, jnp.float32))
        return from_blocks(dense, nr, nc)

    up_whole = rebuild(got_up, masks_up, where_is)
    features3 = features.reshape((features.shape[0], n_row * nr, block))
    cot3 = cot_rows.reshape((cot_rows.shape[0], n_row * nr, block))

    def forward(rows3, w4):
        out = lax.dot_general(
            rows3, w4, (((1, 2), (0, 2)), ((), ())), preferred_element_type=jnp.float32
        )
        return out.reshape((out.shape[0], nc * block))

    def grad_view(rows3, acts):
        acts3 = acts.reshape((acts.shape[0], nc, block))
        out = lax.dot_general(
            rows3, acts3, (((0,), (0,)), ((), ())), preferred_element_type=jnp.float32
        )
        return out.reshape((n_row * nr * block, nc * block))

    preact = forward(features3, up_whole)
    gelu_value, gelu_slope = gelu_parts(preact)
    activation = gelu_value.astype(jnp.bfloat16)
    sent_down = kept_blocks(grad_view(cot3, activation), masks_down, rows_n, 0, slots)
    got_down, sent_down = lax.optimization_barrier((got_down, sent_down))
    summed_down = lax.psum_scatter(sent_down, "row", scatter_dimension=0, tiled=True)[0]

    down_whole = rebuild(got_down.reshape((n_row * width, block, block)), masks_down, in_order)
    act_grad = forward(cot3, down_whole)
    pre_grad = (act_grad * gelu_slope).astype(jnp.bfloat16)
    partial_tokens = lax.dot_general(
        pre_grad.reshape((pre_grad.shape[0], nc, block)),
        up_whole,
        (((1, 2), (1, 3)), ((), ())),
        preferred_element_type=jnp.float32,
    ).reshape((pre_grad.shape[0], n_row * nr * block))
    tokens_part = partial_tokens.astype(jnp.bfloat16)
    summed_up, (summed_down, tokens_part) = ring_reduce(
        grad_view(features3, pre_grad), masks_up, (summed_down, tokens_part)
    )
    grad_down = unpack(summed_down.astype(jnp.float32), flat_down)
    grad_up = unpack(summed_up, flat_up)

    token_grad = lax.psum_scatter(tokens_part, "col", scatter_dimension=1, tiled=True)
    new_up, new_moment_up, new_second_up = adam_update(w_up, moment_up, second_up, grad_up)
    new_down, new_moment_down, new_second_down = adam_update(
        w_down, moment_down, second_down, grad_down
    )
    return (
        token_grad,
        new_up,
        new_moment_up,
        new_second_up,
        new_down,
        new_moment_down,
        new_second_down,
    )


def solution(mesh):
    spec = P("row", "col")
    return jax.shard_map(
        functools.partial(shards, row_ring(mesh)),
        mesh=mesh,
        in_specs=(spec,) * 10,
        out_specs=(spec,) * 7,
        check_vma=False,
    )
```

```python
import functools

import jax
import jax.numpy as jnp
from jax import lax
from jax.sharding import PartitionSpec as P

inv_root_two = 0.7071067811865476
inv_root_two_pi = 0.3989422804014327
learn_rate = 0.001
bias_first = 1.0 - 0.9**10
bias_second = 1.0 - 0.95**10


def expand_mask(mask, block):
    blocks_r, blocks_c = mask.shape
    values = mask.astype(jnp.float32)[:, None, :, None]
    values = jnp.broadcast_to(values, (blocks_r, block, blocks_c, block))
    return values.reshape(blocks_r * block, blocks_c * block)


def gelu_parts(preact):
    normal_cdf = 0.5 * (1.0 + lax.erf(preact * inv_root_two))
    density = jnp.exp(-0.5 * preact * preact) * inv_root_two_pi
    return (preact * normal_cdf, normal_cdf + preact * density)


def adam_update(weight, moment, second, grad):
    moment_new = 0.9 * moment + 0.1 * grad
    second_new = 0.95 * second + 0.05 * grad * grad
    step_size = moment_new / bias_first / (jnp.sqrt(second_new / bias_second) + 1e-08)
    return (weight - learn_rate * step_size, moment_new, second_new)


def token_product(rows_full, other):
    return lax.dot_general(
        rows_full, other, (((0,), (0,)), ((), ())), preferred_element_type=jnp.float32
    )


def to_blocks(dense, block):
    rows, cols = dense.shape[-2:]
    lead = dense.shape[:-2]
    nr, nc = rows // block, cols // block
    x = dense.reshape(lead + (nr, block, nc, block))
    k = len(lead)
    x = jnp.moveaxis(x, k + 2, k + 1)
    return x.reshape(lead + (nr * nc, block, block))


def from_blocks(blocks, nr, nc):
    lead = blocks.shape[:-3]
    block = blocks.shape[-1]
    x = blocks.reshape(lead + (nr, nc, block, block))
    k = len(lead)
    x = jnp.moveaxis(x, k + 1, k + 2)
    return x.reshape(lead + (nr * block, nc * block))


def kept_index(flat_mask, slots):
    n = flat_mask.shape[-1]
    upto = jnp.cumsum(flat_mask, axis=-1)
    k = jnp.arange(slots, dtype=jnp.int32)
    idx = jnp.sum((upto[..., None, :] <= k[:, None]).astype(jnp.int32), axis=-1)
    return jnp.minimum(idx, n - 1)


def slot_of(flat_mask):
    return jnp.cumsum(flat_mask, axis=-1) - flat_mask


def row_ring(mesh):
    devices = mesh.devices
    n = devices.shape[0]
    try:
        pts = [tuple(devices[r, 0].coords) for r in range(n)]
    except AttributeError:
        return list(range(n))

    def near(a, b):
        return sum(abs(i - j) for i, j in zip(pts[a], pts[b])) == 1

    path, used, budget = [0], {0}, [20000]

    def search():
        budget[0] -= 1
        if budget[0] < 0:
            return False
        if len(path) == n:
            return near(path[-1], 0)
        options = [j for j in range(n) if j not in used and near(path[-1], j)]
        options.sort(key=lambda j: sum(1 for k in range(n) if k not in used and near(j, k)))
        for j in options:
            path.append(j)
            used.add(j)
            if search():
                return True
            path.pop()
            used.discard(j)
        return False

    if n > 2 and search():
        return path
    return list(range(n))


def shards(
    ring,
    tokens,
    cotangent,
    w_up,
    w_down,
    mask_up,
    mask_down,
    moment_up,
    second_up,
    moment_down,
    second_down,
):
    nr, nc = mask_up.shape
    nb = nr * nc
    block = w_up.shape[0] // nr
    slots = nb // 2
    n_row = lax.axis_size("row")
    width = slots + 2
    width += width % 2
    zero_slot = slots
    mask_slot = slots + 1
    half = width // 2
    rows_n = jnp.arange(n_row, dtype=jnp.int32)

    place = [0] * n_row
    for i, r in enumerate(ring):
        place[r] = i
    right = [(ring[i], ring[(i + 1) % n_row]) for i in range(n_row)]
    left = [(ring[i], ring[(i - 1) % n_row]) for i in range(n_row)]
    me = lax.axis_index("row")
    place_of = jnp.array(place, jnp.int32)
    ring_of = jnp.array(ring, jnp.int32)
    p = place_of[me]

    flat_up = mask_up.reshape(nb)
    flat_down = mask_down.reshape(nb)

    def package(w, flat):
        blocks = to_blocks(w.astype(jnp.bfloat16), block)
        kept = blocks.at[kept_index(flat, slots)].get(mode="promise_in_bounds")
        extra = jnp.zeros((width - slots, block, block), jnp.bfloat16)
        extra = extra.at[mask_slot - slots, 0, :nb].set(flat_up.astype(jnp.bfloat16))
        extra = extra.at[mask_slot - slots, 1, :nb].set(flat_down.astype(jnp.bfloat16))
        return jnp.concatenate([kept, extra], axis=0)

    def ring_gather(pk):
        a, b = pk[:half], pk[half:]
        got_a, got_b = [a], [b]
        for _ in range(1, n_row):
            a = lax.ppermute(a, "row", right)
            b = lax.ppermute(b, "row", left)
            got_a.append(a)
            got_b.append(b)
        return jnp.stack(got_a + got_b).reshape((2 * n_row * half, block, block))

    q = place_of
    step_a = (p - q) % n_row
    step_b = (q - p) % n_row

    def where_is(k):
        in_a = k < half
        return jnp.where(
            in_a,
            step_a[:, None] * half + k,
            n_row * half + step_b[:, None] * half + (k - half),
        )

    got_up = ring_gather(package(w_up, flat_up))
    got_up, package_down = lax.optimization_barrier((got_up, package(w_down, flat_down)))
    got_down = lax.all_gather(package_down, "row", axis=0)
    mask_blocks = got_up.at[where_is(jnp.full((n_row, 1), mask_slot, jnp.int32))[:, 0]].get(
        mode="promise_in_bounds"
    )
    masks_up = mask_blocks[:, 0, :nb].astype(jnp.int32)
    masks_down = mask_blocks[:, 1, :nb].astype(jnp.int32)

    features, cot_rows = (
        lax.all_gather(tokens, "col", axis=1, tiled=True),
        lax.all_gather(cotangent, "col", axis=1, tiled=True),
    )

    def rebuild(got, masks, at):
        k = jnp.where(masks > 0, slot_of(masks), zero_slot)
        dense = got.at[at(k).reshape(-1)].get(mode="promise_in_bounds")
        return dense.reshape((n_row * nr, nc, block, block))

    def in_order(k):
        return (rows_n * width)[:, None] + k

    def kept_blocks(partial, masks, dest, lo, hi):
        view = partial.astype(jnp.bfloat16).reshape((n_row * nr, block, nc, block))
        idx = kept_index(masks[dest], slots)[:, lo:hi]
        rows = (dest * nr)[:, None] + idx // nc
        cols = idx % nc
        return view.at[rows, :, cols, :].get(mode="promise_in_bounds")

    def ring_reduce(partial, masks, hold=None):
        ha = (slots + 1) // 2
        dest_a = ring_of[(p - rows_n) % n_row]
        dest_b = ring_of[(p + rows_n) % n_row]
        sent_a = kept_blocks(partial, masks, dest_a, 0, ha)
        sent_b = kept_blocks(partial, masks, dest_b, ha, slots)
        if hold is not None:
            hold, sent_a, sent_b = lax.optimization_barrier((hold, sent_a, sent_b))
        acc_a, acc_b = sent_a[1], sent_b[1]
        for s in range(1, n_row):
            in_a = lax.ppermute(acc_a, "row", right).astype(jnp.float32)
            in_b = lax.ppermute(acc_b, "row", left).astype(jnp.float32)
            if s < n_row - 1:
                acc_a = (in_a + sent_a[s + 1].astype(jnp.float32)).astype(jnp.bfloat16)
                acc_b = (in_b + sent_b[s + 1].astype(jnp.float32)).astype(jnp.bfloat16)
        total_a = in_a + sent_a[0].astype(jnp.float32)
        total_b = in_b + sent_b[0].astype(jnp.float32)
        return jnp.concatenate([total_a, total_b], axis=0), hold

    def unpack(summed, own):
        dense = summed.at[slot_of(own)].get(mode="promise_in_bounds")
        keep = own[:, None, None] > 0
        dense = jnp.where(keep, dense, jnp.zeros(dense.shape, jnp.float32))
        return from_blocks(dense, nr, nc)

    up_whole = rebuild(got_up, masks_up, where_is)
    features3 = features.reshape((features.shape[0], n_row * nr, block))
    cot3 = cot_rows.reshape((cot_rows.shape[0], n_row * nr, block))

    def forward(rows3, w4):
        out = lax.dot_general(
            rows3, w4, (((1, 2), (0, 2)), ((), ())), preferred_element_type=jnp.float32
        )
        return out.reshape((out.shape[0], nc * block))

    def grad_view(rows3, acts):
        acts3 = acts.reshape((acts.shape[0], nc, block))
        out = lax.dot_general(
            rows3, acts3, (((0,), (0,)), ((), ())), preferred_element_type=jnp.float32
        )
        return out.reshape((n_row * nr * block, nc * block))

    preact = forward(features3, up_whole)
    gelu_value, gelu_slope = gelu_parts(preact)
    activation = gelu_value.astype(jnp.bfloat16)
    sent_down = kept_blocks(grad_view(cot3, activation), masks_down, rows_n, 0, slots)
    got_down, sent_down = lax.optimization_barrier((got_down, sent_down))
    summed_down = lax.psum_scatter(sent_down, "row", scatter_dimension=0, tiled=True)[0]

    down_whole = rebuild(got_down.reshape((n_row * width, block, block)), masks_down, in_order)
    act_grad = forward(cot3, down_whole)
    pre_grad = (act_grad * gelu_slope).astype(jnp.bfloat16)
    partial_tokens = lax.dot_general(
        pre_grad.reshape((pre_grad.shape[0], nc, block)),
        up_whole,
        (((1, 2), (1, 3)), ((), ())),
        preferred_element_type=jnp.float32,
    ).reshape((pre_grad.shape[0], n_row * nr * block))
    tokens_part = partial_tokens.astype(jnp.bfloat16)
    summed_up, (summed_down, tokens_part) = ring_reduce(
        grad_view(features3, pre_grad), masks_up, (summed_down, tokens_part)
    )
    grad_down = unpack(summed_down.astype(jnp.float32), flat_down)
    grad_up = unpack(summed_up, flat_up)

    token_grad = lax.psum_scatter(tokens_part, "col", scatter_dimension=1, tiled=True)
    new_up, new_moment_up, new_second_up = adam_update(w_up, moment_up, second_up, grad_up)
    new_down, new_moment_down, new_second_down = adam_update(
        w_down, moment_down, second_down, grad_down
    )
    return (
        token_grad,
        new_up,
        new_moment_up,
        new_second_up,
        new_down,
        new_moment_down,
        new_second_down,
    )


def solution(mesh):
    spec = P("row", "col")
    return jax.shard_map(
        functools.partial(shards, row_ring(mesh)),
        mesh=mesh,
        in_specs=(spec,) * 10,
        out_specs=(spec,) * 7,
        check_vma=False,
    )
```
